128 devices in a mesh: chan: 32 (over y, z, x_lo), tm: 4 (over x_hi, core).
Axes of the slice: x: 4 (x_hi: 2, x_lo: 2; x = x_hi * 2 + x_lo), y: 4, z: 4, core: 2. Of those that a mesh axis runs over, the one named last changes fastest.
Arguments:
- record: float32 [64, 256, 16384], P('tm', 'chan'), may hold values from -6 to 6
- fir_taps: float32 [64], replicated, may hold values from -0.75 to 0.75
- pair_offsets: int32 [8], replicated, may hold values from -128 to 128, as said below
Outputs:
- correlation: float32 [8, 256, 16384], P('tm', None, 'chan')
The draws below stay inside these ranges and needn't reach their ends.
Inputs may be any that keep to these rules, and one draw needn't show every extreme that they name: `pair_offsets`: 8 distinct nonzero channel offsets; both -128 and 128 are among them.
All inputs are finite; a program needn't handle non-finite values.
Results may differ from the reference program's by a relative error of at most 0.000098.
Values sent between devices are 32-bit elements; how exact they have to be, the bound alone decides.
No kernel may reach another device: no remote copies, remote signals or barrier semaphores. Data moves between devices by JAX's collectives and lax.ppermute only.
A program may use at most 192 MiB of HBM per device.

```python
import math
import jax
import jax.numpy as jnp
from jax import lax

C = 16384
S = 256
TAPS = 64
R = 128
K = 8
SEGS = 64
HALF = 128


def draw_pair_offsets(key, part):
    shuffled = jax.random.permutation(key, 2 * R - 2)
    interior = shuffled[:K - 2] + 1
    interior = jnp.where(interior <= R - 1, interior, R - 1 - interior)
    extremes = jnp.array([-R, R], dtype=jnp.int32)
    merged = jnp.concatenate([extremes, interior.astype(jnp.int32)])
    return jax.random.permutation(jax.random.fold_in(key, 7), merged)


def levels(key, dims, shards, smallest, largest):
    loudness, own = 1.0, jax.random.fold_in(key, 6)
    for position, blocks in shards:
        steps = jnp.exp(jax.random.uniform(jax.random.fold_in(own, position), (blocks,), jnp.float32, smallest / len(shards), largest / len(shards)))
        loudness = loudness * jnp.repeat(steps, dims[position] // blocks).reshape([-1 if axis == position else 1 for axis in range(len(dims))])
    return loudness


def noise(key, shape, scale, limit, pieces=(), held_as=jnp.bfloat16):
    result = scale * jax.random.normal(key, shape, jnp.float32)
    if pieces:
        result = result * levels(key, shape, pieces, -0.22, 0.18)
    return jnp.clip(result, -limit, limit).astype(held_as)


def setup_inputs(seed: int = 0) -> dict:
    streams_of = jax.random.split(jax.random.key(seed), 4)
    return {
        "record": noise(streams_of[0], (SEGS, S, C), 1.0, 6.0, ((0, 4), (1, 32)), jnp.float32),
        "fir_taps": noise(streams_of[1], (TAPS,), TAPS ** -0.5, 0.75, (), jnp.float32),
        "pair_offsets": draw_pair_offsets(jax.random.fold_in(streams_of[3], 71), 0),
    }


def reference(record, fir_taps, pair_offsets):
    length = 2 * S
    tap_spec = jnp.fft.rfft(fir_taps, n=length)
    raw_spec = jnp.fft.rfft(record, n=length, axis=1)
    whitened = jnp.fft.irfft(raw_spec * tap_spec[None, :, None], n=length, axis=1)[:, :S, :]
    spectra = jnp.fft.rfft(whitened, n=length, axis=1)
    norm_scale = 1.0 / math.sqrt(SEGS * S)

    def one_offset(offset):
        partner = jnp.roll(spectra, -offset, axis=2)
        cross_spec = lax.optimization_barrier(jnp.sum(jnp.conj(spectra) * partner, axis=0))
        circular = jnp.fft.irfft(cross_spec, n=length, axis=0)
        return jnp.concatenate([circular[length - HALF:], circular[:HALF]], axis=0) * norm_scale
    return lax.map(one_offset, pair_offsets).astype(jnp.float32)
```

```python
import math

import jax
import jax.numpy as jnp
from jax import lax
from jax.sharding import PartitionSpec as P

S = 256
R = 128


PRECISE = lax.Precision.HIGHEST
FAST = lax.Precision.HIGH


def fir_matrix_of(fir_taps, seg_len):
    row_ids = lax.broadcasted_iota(jnp.int32, (seg_len, seg_len), 0)
    col_ids = lax.broadcasted_iota(jnp.int32, (seg_len, seg_len), 1)
    spread = col_ids - row_ids
    taps = fir_taps.shape[0]
    picked = jnp.take(fir_taps, jnp.clip(spread, 0, taps - 1), axis=0)
    return jnp.where((spread >= 0) & (spread < taps), picked, 0.0)


def forward_table(seg_len):
    length = 2 * seg_len
    time_ids = lax.broadcasted_iota(jnp.int32, (seg_len, length), 0)
    slot_ids = lax.broadcasted_iota(jnp.int32, (seg_len, length), 1)
    frequency = jnp.where(slot_ids <= seg_len, slot_ids, slot_ids - seg_len)
    angles = (frequency * time_ids % length).astype(jnp.float32) * (2.0 * math.pi / length)
    return jnp.where(slot_ids <= seg_len, jnp.cos(angles), jnp.sin(angles))


def inverse_table(seg_len, norm_scale):
    length = 2 * seg_len
    slot_ids = lax.broadcasted_iota(jnp.int32, (3 * seg_len, seg_len), 0)
    lag_ids = lax.broadcasted_iota(jnp.int32, (3 * seg_len, seg_len), 1) - seg_len // 2
    cosine_rows = slot_ids < length
    frequency = jnp.where(
        cosine_rows, jnp.where(slot_ids <= seg_len, slot_ids, slot_ids - seg_len), slot_ids - length
    )
    angles = (frequency * lag_ids % length).astype(jnp.float32) * (2.0 * math.pi / length)
    edge_rows = (slot_ids == 0) | (slot_ids == seg_len)
    cosine_weights = jnp.where(edge_rows, 1.0 / length, 2.0 / length)
    sine_weights = jnp.where(frequency == 0, 0.0, -2.0 / length)
    values = jnp.where(
        cosine_rows, cosine_weights * jnp.cos(angles), sine_weights * jnp.sin(angles)
    )
    return values * norm_scale


def halo(array, axis, dim, width):
    size, length = (lax.axis_size(axis), array.shape[dim])
    up = [(i, (i + 1) % size) for i in range(size)]
    down = [(j, i) for i, j in up]
    last = lax.slice_in_dim(array, length - width, length, axis=dim)
    first = lax.slice_in_dim(array, 0, width, axis=dim)
    before = lax.ppermute(last, axis, up)
    after = lax.ppermute(first, axis, down)
    return jnp.concatenate([before, array, after], axis=dim)


def per_device(record, fir_taps, pair_offsets):
    n_chan = lax.axis_size("chan")
    n_time = lax.axis_size("tm")
    seg_count, part_rows, channels = record.shape
    block_width = channels // n_chan
    table = jnp.dot(fir_matrix_of(fir_taps, S), forward_table(S), precision=PRECISE)
    table = table.reshape(n_chan, part_rows, 2 * S)
    pieces = record.reshape(seg_count, part_rows, n_chan, block_width).transpose(2, 0, 1, 3)
    turned = lax.all_to_all(pieces, "chan", split_axis=0, concat_axis=0, tiled=True)
    widened = halo(turned, "chan", 3, R)
    spectra = jnp.einsum("asuc,auj->scj", widened, table, precision=FAST)
    own_spec = spectra[:, R : R + block_width, :]
    norm_scale = 1.0 / math.sqrt(seg_count * n_time * S)
    inverse = inverse_table(S, norm_scale)
    inverse_cos = inverse[: 2 * S]
    inverse_sin = inverse[2 * S :]
    inverse_all = jnp.concatenate([inverse_cos, -inverse_sin, inverse_sin], axis=0)

    def one_offset(offset):
        partner = lax.dynamic_slice_in_dim(spectra, R + offset, block_width, axis=1)
        swapped = jnp.roll(partner, S, axis=2)
        both = jnp.concatenate([own_spec * partner, own_spec * swapped], axis=2)
        summed = jnp.sum(both, axis=0)
        return jnp.einsum("cr,rl->lc", summed, inverse_all, precision=FAST)

    even = lax.map(one_offset, pair_offsets[0::2])
    first = lax.psum_scatter(even, "tm", scatter_dimension=0, tiled=True)
    odd = lax.map(one_offset, pair_offsets[1::2])
    second = lax.psum_scatter(odd, "tm", scatter_dimension=0, tiled=True)
    return jnp.concatenate([first, second], axis=0)


def solution(mesh):
    placed = (P("tm", "chan", None), P(), P())
    return jax.shard_map(
        per_device, mesh=mesh, in_specs=placed, out_specs=P("tm", None, "chan"), check_vma=False
    )
```

```python
import math

import jax
import jax.numpy as jnp
from jax import lax
from jax.experimental import pallas as pl
from jax.experimental.pallas import tpu as pltpu
from jax.sharding import PartitionSpec as P

S = 256
R = 128


PRECISE = lax.Precision.HIGHEST
FAST = lax.Precision.HIGH


def fir_matrix_of(fir_taps, seg_len):
    row_ids = lax.broadcasted_iota(jnp.int32, (seg_len, seg_len), 0)
    col_ids = lax.broadcasted_iota(jnp.int32, (seg_len, seg_len), 1)
    spread = col_ids - row_ids
    tap_ids = lax.broadcasted_iota(jnp.int32, (1, 1, fir_taps.shape[0]), 2)
    hits = spread[:, :, None] == tap_ids
    return jnp.sum(jnp.where(hits, fir_taps[None, None, :], 0.0), axis=2)


def forward_table(seg_len):
    length = 2 * seg_len
    time_ids = lax.broadcasted_iota(jnp.int32, (seg_len, length), 0)
    slot_ids = lax.broadcasted_iota(jnp.int32, (seg_len, length), 1)
    frequency = jnp.where(slot_ids <= seg_len, slot_ids, slot_ids - seg_len)
    angles = (frequency * time_ids % length).astype(jnp.float32) * (2.0 * math.pi / length)
    return jnp.where(slot_ids <= seg_len, jnp.cos(angles), jnp.sin(angles))


def inverse_table(seg_len, norm_scale):
    length = 2 * seg_len
    slot_ids = lax.broadcasted_iota(jnp.int32, (3 * seg_len, seg_len), 0)
    lag_ids = lax.broadcasted_iota(jnp.int32, (3 * seg_len, seg_len), 1) - seg_len // 2
    cosine_rows = slot_ids < length
    frequency = jnp.where(
        cosine_rows, jnp.where(slot_ids <= seg_len, slot_ids, slot_ids - seg_len), slot_ids - length
    )
    angles = (frequency * lag_ids % length).astype(jnp.float32) * (2.0 * math.pi / length)
    edge_rows = (slot_ids == 0) | (slot_ids == seg_len)
    cosine_weights = jnp.where(edge_rows, 1.0 / length, 2.0 / length)
    sine_weights = jnp.where(frequency == 0, 0.0, -2.0 / length)
    values = jnp.where(
        cosine_rows, cosine_weights * jnp.cos(angles), sine_weights * jnp.sin(angles)
    )
    return values * norm_scale


def halo(array, axis, dim, width):
    size, length = (lax.axis_size(axis), array.shape[dim])
    up = [(i, (i + 1) % size) for i in range(size)]
    down = [(j, i) for i, j in up]
    last = lax.slice_in_dim(array, length - width, length, axis=dim)
    first = lax.slice_in_dim(array, 0, width, axis=dim)
    before = lax.ppermute(last, axis, up)
    after = lax.ppermute(first, axis, down)
    return jnp.concatenate([before, array, after], axis=dim)


def cross_kernel(offs_ref, spec_ref, out_ref):
    segs, ext, width = spec_ref.shape
    half = width // 2
    start = R + offs_ref[pl.program_id(0)]
    rem = start % 8
    base = start - rem
    turn = (8 - rem) % 8
    keep = lax.broadcasted_iota(jnp.int32, (8, width), 0) < 8 - rem

    def body(r, carry):
        r0 = pl.multiple_of(R + r * 8, 8)
        p0 = pl.multiple_of(base + r * 8, 8)
        p1 = pl.multiple_of(jnp.minimum(p0 + 8, ext - 8), 8)
        acc_m = jnp.zeros((8, width), jnp.float32)
        acc_lo = jnp.zeros((8, half), jnp.float32)
        acc_hi = jnp.zeros((8, half), jnp.float32)
        for s in range(segs):
            a = spec_ref[s, pl.ds(r0, 8), :]
            b0 = pltpu.roll(spec_ref[s, pl.ds(p0, 8), :], turn, 0)
            b1 = pltpu.roll(spec_ref[s, pl.ds(p1, 8), :], turn, 0)
            b = jnp.where(keep, b0, b1)
            acc_m = acc_m + a * b
            acc_lo = acc_lo + a[:, :half] * b[:, half:]
            acc_hi = acc_hi + a[:, half:] * b[:, :half]
        o0 = pl.multiple_of(r * 8, 8)
        out_ref[pl.ds(o0, 8), 0:width] = acc_m
        out_ref[pl.ds(o0, 8), width:] = acc_hi - acc_lo
        return carry

    lax.fori_loop(0, (ext - 2 * R) // 8, body, 0, unroll=2)


def cross_spectra(spectra, offsets):
    segs, ext, width = spectra.shape
    own_w = ext - 2 * R
    n_k = offsets.shape[0]
    out_w = width + width // 2
    grid_spec = pltpu.PrefetchScalarGridSpec(
        num_scalar_prefetch=1,
        grid=(n_k,),
        in_specs=[
            pl.BlockSpec(
                (segs, ext, width), lambda k, offs: (0, 0, 0), pipeline_mode=pl.Buffered(1)
            ),
        ],
        out_specs=pl.BlockSpec((None, own_w, out_w), lambda k, offs: (k, 0, 0)),
    )
    return pl.pallas_call(
        cross_kernel,
        grid_spec=grid_spec,
        out_shape=jax.ShapeDtypeStruct((n_k, own_w, out_w), jnp.float32),
        compiler_params=pltpu.CompilerParams(
            dimension_semantics=("arbitrary",), vmem_limit_bytes=48 * 1024 * 1024
        ),
    )(offsets, spectra)


def per_device(record, fir_taps, pair_offsets):
    n_chan = lax.axis_size("chan")
    n_time = lax.axis_size("tm")
    seg_count, part_rows, channels = record.shape
    block_width = channels // n_chan
    table = jnp.dot(fir_matrix_of(fir_taps, S), forward_table(S), precision=PRECISE)
    table = table.reshape(n_chan, part_rows, 2 * S)
    pieces = record.reshape(seg_count, part_rows, n_chan, block_width).transpose(2, 0, 1, 3)
    turned = lax.all_to_all(pieces, "chan", split_axis=0, concat_axis=0, tiled=True)
    widened = halo(turned, "chan", 3, R)
    spectra = jnp.einsum("asuc,auj->scj", widened, table, precision=FAST)
    norm_scale = 1.0 / math.sqrt(seg_count * n_time * S)
    inverse = inverse_table(S, norm_scale)
    inverse_cat = jnp.concatenate([inverse[: 2 * S], inverse[2 * S :]], axis=0)

    def some_offsets(offsets):
        crossed = cross_spectra(spectra, offsets)
        lagged = jnp.einsum("kcr,rl->klc", crossed, inverse_cat, precision=FAST)
        return lax.psum_scatter(lagged, "tm", scatter_dimension=0, tiled=True)

    first = some_offsets(pair_offsets[0::2])
    second = some_offsets(pair_offsets[1::2])
    return jnp.concatenate([first, second], axis=0)


def solution(mesh):
    placed = (P("tm", "chan", None), P(), P())
    return jax.shard_map(
        per_device, mesh=mesh, in_specs=placed, out_specs=P("tm", None, "chan"), check_vma=False
    )
```

```python
import math

import jax
import jax.numpy as jnp
from jax import lax
from jax.experimental import pallas as pl
from jax.experimental.pallas import tpu as pltpu
from jax.sharding import PartitionSpec as P

S = 256
R = 128


PRECISE = lax.Precision.HIGHEST
FAST = lax.Precision.HIGH


def fir_matrix_of(fir_taps, seg_len):
    row_ids = lax.broadcasted_iota(jnp.int32, (seg_len, seg_len), 0)
    col_ids = lax.broadcasted_iota(jnp.int32, (seg_len, seg_len), 1)
    spread = col_ids - row_ids
    tap_ids = lax.broadcasted_iota(jnp.int32, (1, 1, fir_taps.shape[0]), 2)
    hits = spread[:, :, None] == tap_ids
    return jnp.sum(jnp.where(hits, fir_taps[None, None, :], 0.0), axis=2)


def forward_table(seg_len):
    length = 2 * seg_len
    time_ids = lax.broadcasted_iota(jnp.int32, (seg_len, length), 0)
    slot_ids = lax.broadcasted_iota(jnp.int32, (seg_len, length), 1)
    frequency = jnp.where(slot_ids <= seg_len, slot_ids, slot_ids - seg_len)
    angles = (frequency * time_ids % length).astype(jnp.float32) * (2.0 * math.pi / length)
    return jnp.where(slot_ids <= seg_len, jnp.cos(angles), jnp.sin(angles))


def inverse_table(seg_len, norm_scale):
    length = 2 * seg_len
    slot_ids = lax.broadcasted_iota(jnp.int32, (3 * seg_len, seg_len), 0)
    lag_ids = lax.broadcasted_iota(jnp.int32, (3 * seg_len, seg_len), 1) - seg_len // 2
    cosine_rows = slot_ids < length
    frequency = jnp.where(
        cosine_rows, jnp.where(slot_ids <= seg_len, slot_ids, slot_ids - seg_len), slot_ids - length
    )
    angles = (frequency * lag_ids % length).astype(jnp.float32) * (2.0 * math.pi / length)
    edge_rows = (slot_ids == 0) | (slot_ids == seg_len)
    cosine_weights = jnp.where(edge_rows, 1.0 / length, 2.0 / length)
    sine_weights = jnp.where(frequency == 0, 0.0, -2.0 / length)
    values = jnp.where(
        cosine_rows, cosine_weights * jnp.cos(angles), sine_weights * jnp.sin(angles)
    )
    return values * norm_scale


def halo(array, axis, dim, width):
    size, length = (lax.axis_size(axis), array.shape[dim])
    up = [(i, (i + 1) % size) for i in range(size)]
    down = [(j, i) for i, j in up]
    last = lax.slice_in_dim(array, length - width, length, axis=dim)
    first = lax.slice_in_dim(array, 0, width, axis=dim)
    before = lax.ppermute(last, axis, up)
    after = lax.ppermute(first, axis, down)
    return jnp.concatenate([before, array, after], axis=dim)


CHUNKS = 4


def cross_kernel(offs_ref, spec_ref, acc_ref, out_ref):
    segs, ext, width = spec_ref.shape
    half = width // 2
    start = R + offs_ref[pl.program_id(0)]
    rem = start % 8
    base = start - rem
    turn = (8 - rem) % 8
    keep = lax.broadcasted_iota(jnp.int32, (8, width), 0) < 8 - rem

    def body(r, carry):
        r0 = pl.multiple_of(R + r * 8, 8)
        p0 = pl.multiple_of(base + r * 8, 8)
        p1 = pl.multiple_of(jnp.minimum(p0 + 8, ext - 8), 8)
        o0 = pl.multiple_of(r * 8, 8)
        acc_m = acc_ref[pl.ds(o0, 8), 0:width]
        acc_lo = jnp.zeros((8, half), jnp.float32)
        acc_hi = acc_ref[pl.ds(o0, 8), width:]
        for s in range(segs):
            a = spec_ref[s, pl.ds(r0, 8), :]
            b0 = pltpu.roll(spec_ref[s, pl.ds(p0, 8), :], turn, 0)
            b1 = pltpu.roll(spec_ref[s, pl.ds(p1, 8), :], turn, 0)
            b = jnp.where(keep, b0, b1)
            acc_m = acc_m + a * b
            acc_lo = acc_lo + a[:, :half] * b[:, half:]
            acc_hi = acc_hi + a[:, half:] * b[:, :half]
        out_ref[pl.ds(o0, 8), 0:width] = acc_m
        out_ref[pl.ds(o0, 8), width:] = acc_hi - acc_lo
        return carry

    lax.fori_loop(0, (ext - 2 * R) // 8, body, 0, unroll=2)


def cross_spectra(spectra, offsets, acc):
    segs, ext, width = spectra.shape
    n_k, own_w, out_w = acc.shape
    grid_spec = pltpu.PrefetchScalarGridSpec(
        num_scalar_prefetch=1,
        grid=(n_k,),
        in_specs=[
            pl.BlockSpec(
                (segs, ext, width), lambda k, offs: (0, 0, 0), pipeline_mode=pl.Buffered(1)
            ),
            pl.BlockSpec((None, own_w, out_w), lambda k, offs: (k, 0, 0)),
        ],
        out_specs=pl.BlockSpec((None, own_w, out_w), lambda k, offs: (k, 0, 0)),
    )
    return pl.pallas_call(
        cross_kernel,
        grid_spec=grid_spec,
        out_shape=jax.ShapeDtypeStruct(acc.shape, jnp.float32),
        input_output_aliases={2: 0},
        compiler_params=pltpu.CompilerParams(
            dimension_semantics=("arbitrary",), vmem_limit_bytes=48 * 1024 * 1024
        ),
    )(offsets, spectra, acc)


def windows(piece, n_chan, width):
    segs, rows, channels = piece.shape
    blocks = piece.reshape(segs, rows, n_chan, channels // n_chan)
    before = jnp.roll(blocks, 1, axis=2)[..., -width:]
    after = jnp.roll(blocks, -1, axis=2)[..., :width]
    return jnp.concatenate([before, blocks, after], axis=3).transpose(2, 0, 1, 3)


def per_device(record, fir_taps, pair_offsets):
    n_chan = lax.axis_size("chan")
    n_time = lax.axis_size("tm")
    seg_count, part_rows, channels = record.shape
    block_width = channels // n_chan
    table = jnp.dot(fir_matrix_of(fir_taps, S), forward_table(S), precision=PRECISE)
    table = table.reshape(n_chan, part_rows, 2 * S)
    norm_scale = 1.0 / math.sqrt(seg_count * n_time * S)
    inverse = inverse_table(S, norm_scale)
    inverse_cat = jnp.concatenate([inverse[: 2 * S], inverse[2 * S :]], axis=0)
    even_offsets = pair_offsets[0::2]
    odd_offsets = pair_offsets[1::2]
    acc_shape = (even_offsets.shape[0], block_width, 3 * S)
    even = jnp.zeros(acc_shape, jnp.float32)
    odd = jnp.zeros(acc_shape, jnp.float32)
    step = seg_count // CHUNKS
    for g in range(CHUNKS):
        piece = windows(record[g * step : (g + 1) * step], n_chan, R)
        turned = lax.all_to_all(piece, "chan", split_axis=0, concat_axis=0, tiled=True)
        spectra = jnp.einsum("asuc,auj->scj", turned, table, precision=FAST)
        even = cross_spectra(spectra, even_offsets, even)
        odd = cross_spectra(spectra, odd_offsets, odd)

    def finish(crossed):
        lagged = jnp.einsum("kcr,rl->klc", crossed, inverse_cat, precision=FAST)
        return lax.psum_scatter(lagged, "tm", scatter_dimension=0, tiled=True)

    first = finish(even)
    second = finish(odd)
    return jnp.concatenate([first, second], axis=0)


def solution(mesh):
    placed = (P("tm", "chan", None), P(), P())
    return jax.shard_map(
        per_device, mesh=mesh, in_specs=placed, out_specs=P("tm", None, "chan"), check_vma=False
    )
```

```python
import math

import jax
import jax.numpy as jnp
from jax import lax
from jax.experimental import pallas as pl
from jax.experimental.pallas import tpu as pltpu
from jax.sharding import PartitionSpec as P

S = 256
R = 128


PRECISE = lax.Precision.HIGHEST
FAST = lax.Precision.HIGH


def fir_matrix_of(fir_taps, seg_len):
    row_ids = lax.broadcasted_iota(jnp.int32, (seg_len, seg_len), 0)
    col_ids = lax.broadcasted_iota(jnp.int32, (seg_len, seg_len), 1)
    spread = col_ids - row_ids
    tap_ids = lax.broadcasted_iota(jnp.int32, (1, 1, fir_taps.shape[0]), 2)
    hits = spread[:, :, None] == tap_ids
    return jnp.sum(jnp.where(hits, fir_taps[None, None, :], 0.0), axis=2)


def forward_table(seg_len):
    length = 2 * seg_len
    time_ids = lax.broadcasted_iota(jnp.int32, (seg_len, length), 0)
    slot_ids = lax.broadcasted_iota(jnp.int32, (seg_len, length), 1)
    frequency = jnp.where(slot_ids <= seg_len, slot_ids, slot_ids - seg_len)
    angles = (frequency * time_ids % length).astype(jnp.float32) * (2.0 * math.pi / length)
    return jnp.where(slot_ids <= seg_len, jnp.cos(angles), jnp.sin(angles))


def inverse_table(seg_len, norm_scale):
    length = 2 * seg_len
    slot_ids = lax.broadcasted_iota(jnp.int32, (3 * seg_len, seg_len), 0)
    lag_ids = lax.broadcasted_iota(jnp.int32, (3 * seg_len, seg_len), 1) - seg_len // 2
    cosine_rows = slot_ids < length
    frequency = jnp.where(
        cosine_rows, jnp.where(slot_ids <= seg_len, slot_ids, slot_ids - seg_len), slot_ids - length
    )
    angles = (frequency * lag_ids % length).astype(jnp.float32) * (2.0 * math.pi / length)
    edge_rows = (slot_ids == 0) | (slot_ids == seg_len)
    cosine_weights = jnp.where(edge_rows, 1.0 / length, 2.0 / length)
    sine_weights = jnp.where(frequency == 0, 0.0, -2.0 / length)
    values = jnp.where(
        cosine_rows, cosine_weights * jnp.cos(angles), sine_weights * jnp.sin(angles)
    )
    return values * norm_scale


def halo(array, axis, dim, width):
    size, length = (lax.axis_size(axis), array.shape[dim])
    up = [(i, (i + 1) % size) for i in range(size)]
    down = [(j, i) for i, j in up]
    last = lax.slice_in_dim(array, length - width, length, axis=dim)
    first = lax.slice_in_dim(array, 0, width, axis=dim)
    before = lax.ppermute(last, axis, up)
    after = lax.ppermute(first, axis, down)
    return jnp.concatenate([before, array, after], axis=dim)


CHUNKS = 4


def cross_kernel(offs_ref, spec_ref, acc_ref, out_ref):
    segs, ext, width = spec_ref.shape
    half = width // 2
    start = R + offs_ref[pl.program_id(0)]
    rem = start % 8
    base = start - rem
    turn = (8 - rem) % 8
    keep = lax.broadcasted_iota(jnp.int32, (8, width), 0) < 8 - rem

    def body(r, carry):
        r0 = pl.multiple_of(R + r * 8, 8)
        p0 = pl.multiple_of(base + r * 8, 8)
        p1 = pl.multiple_of(jnp.minimum(p0 + 8, ext - 8), 8)
        o0 = pl.multiple_of(r * 8, 8)
        acc_m = acc_ref[pl.ds(o0, 8), 0:width]
        acc_lo = jnp.zeros((8, half), jnp.float32)
        acc_hi = acc_ref[pl.ds(o0, 8), width:]
        for s in range(segs):
            a = spec_ref[s, pl.ds(r0, 8), :]
            b0 = pltpu.roll(spec_ref[s, pl.ds(p0, 8), :], turn, 0)
            b1 = pltpu.roll(spec_ref[s, pl.ds(p1, 8), :], turn, 0)
            b = jnp.where(keep, b0, b1)
            acc_m = acc_m + a * b
            acc_lo = acc_lo + a[:, :half] * b[:, half:]
            acc_hi = acc_hi + a[:, half:] * b[:, :half]
        out_ref[pl.ds(o0, 8), 0:width] = acc_m
        out_ref[pl.ds(o0, 8), width:] = acc_hi - acc_lo
        return carry

    lax.fori_loop(0, (ext - 2 * R) // 8, body, 0, unroll=2)


def cross_spectra(spectra, offsets, acc):
    segs, ext, width = spectra.shape
    n_k, own_w, out_w = acc.shape
    grid_spec = pltpu.PrefetchScalarGridSpec(
        num_scalar_prefetch=1,
        grid=(n_k,),
        in_specs=[
            pl.BlockSpec(
                (segs, ext, width), lambda k, offs: (0, 0, 0), pipeline_mode=pl.Buffered(1)
            ),
            pl.BlockSpec((None, own_w, out_w), lambda k, offs: (k, 0, 0)),
        ],
        out_specs=pl.BlockSpec((None, own_w, out_w), lambda k, offs: (k, 0, 0)),
    )
    return pl.pallas_call(
        cross_kernel,
        grid_spec=grid_spec,
        out_shape=jax.ShapeDtypeStruct(acc.shape, jnp.float32),
        input_output_aliases={2: 0},
        compiler_params=pltpu.CompilerParams(
            dimension_semantics=("arbitrary",), vmem_limit_bytes=48 * 1024 * 1024
        ),
    )(offsets, spectra, acc)


def windows(piece, n_chan, width):
    segs, rows, channels = piece.shape
    blocks = piece.reshape(segs, rows, n_chan, channels // n_chan)
    before = jnp.roll(blocks, 1, axis=2)[..., -width:]
    after = jnp.roll(blocks, -1, axis=2)[..., :width]
    return jnp.concatenate([before, blocks, after], axis=3).transpose(2, 0, 1, 3)


def per_device(record, fir_taps, pair_offsets):
    n_chan = lax.axis_size("chan")
    n_time = lax.axis_size("tm")
    seg_count, part_rows, channels = record.shape
    block_width = channels // n_chan
    table = jnp.dot(fir_matrix_of(fir_taps, S), forward_table(S), precision=PRECISE)
    table = table.reshape(n_chan, part_rows, 2 * S)
    norm_scale = 1.0 / math.sqrt(seg_count * n_time * S)
    inverse = inverse_table(S, norm_scale)
    inverse_cat = jnp.concatenate([inverse[: 2 * S], inverse[2 * S :]], axis=0)
    even_offsets = pair_offsets[0::2]
    odd_offsets = pair_offsets[1::2]
    acc_shape = (even_offsets.shape[0], block_width, 3 * S)
    even = jnp.zeros(acc_shape, jnp.float32)
    odd = jnp.zeros(acc_shape, jnp.float32)
    step = seg_count // CHUNKS

    def exchange(g):
        piece = windows(lax.dynamic_slice_in_dim(record, g * step, step, 0), n_chan, R)
        return lax.all_to_all(piece, "chan", split_axis=0, concat_axis=0, tiled=True)

    def accumulate(turned, even, odd):
        spectra = jnp.einsum("asuc,auj->scj", turned, table, precision=FAST)
        return cross_spectra(spectra, even_offsets, even), cross_spectra(spectra, odd_offsets, odd)

    def body(g, carry):
        turned, even, odd = carry
        upcoming = exchange(g + 1)
        even, odd = accumulate(turned, even, odd)
        return upcoming, even, odd

    turned, even, odd = lax.fori_loop(0, CHUNKS - 1, body, (exchange(0), even, odd))
    even, odd = accumulate(turned, even, odd)

    def finish(crossed):
        lagged = jnp.einsum("kcr,rl->klc", crossed, inverse_cat, precision=FAST)
        return lax.psum_scatter(lagged, "tm", scatter_dimension=0, tiled=True)

    first = finish(even)
    second = finish(odd)
    return jnp.concatenate([first, second], axis=0)


def solution(mesh):
    placed = (P("tm", "chan", None), P(), P())
    return jax.shard_map(
        per_device, mesh=mesh, in_specs=placed, out_specs=P("tm", None, "chan"), check_vma=False
    )
```

```python
import math

import jax
import jax.numpy as jnp
from jax import lax
from jax.experimental import pallas as pl
from jax.experimental.pallas import tpu as pltpu
from jax.sharding import PartitionSpec as P

S = 256
R = 128


PRECISE = lax.Precision.HIGHEST
FAST = lax.Precision.HIGH


def fir_matrix_of(fir_taps, seg_len):
    row_ids = lax.broadcasted_iota(jnp.int32, (seg_len, seg_len), 0)
    col_ids = lax.broadcasted_iota(jnp.int32, (seg_len, seg_len), 1)
    spread = col_ids - row_ids
    tap_ids = lax.broadcasted_iota(jnp.int32, (1, 1, fir_taps.shape[0]), 2)
    hits = spread[:, :, None] == tap_ids
    return jnp.sum(jnp.where(hits, fir_taps[None, None, :], 0.0), axis=2)


def forward_table(seg_len):
    length = 2 * seg_len
    time_ids = lax.broadcasted_iota(jnp.int32, (seg_len, length), 0)
    slot_ids = lax.broadcasted_iota(jnp.int32, (seg_len, length), 1)
    frequency = jnp.where(slot_ids <= seg_len, slot_ids, slot_ids - seg_len)
    angles = (frequency * time_ids % length).astype(jnp.float32) * (2.0 * math.pi / length)
    return jnp.where(slot_ids <= seg_len, jnp.cos(angles), jnp.sin(angles))


def inverse_table(seg_len, norm_scale):
    length = 2 * seg_len
    slot_ids = lax.broadcasted_iota(jnp.int32, (3 * seg_len, seg_len), 0)
    lag_ids = lax.broadcasted_iota(jnp.int32, (3 * seg_len, seg_len), 1) - seg_len // 2
    cosine_rows = slot_ids < length
    frequency = jnp.where(
        cosine_rows, jnp.where(slot_ids <= seg_len, slot_ids, slot_ids - seg_len), slot_ids - length
    )
    angles = (frequency * lag_ids % length).astype(jnp.float32) * (2.0 * math.pi / length)
    edge_rows = (slot_ids == 0) | (slot_ids == seg_len)
    cosine_weights = jnp.where(edge_rows, 1.0 / length, 2.0 / length)
    sine_weights = jnp.where(frequency == 0, 0.0, -2.0 / length)
    values = jnp.where(
        cosine_rows, cosine_weights * jnp.cos(angles), sine_weights * jnp.sin(angles)
    )
    return values * norm_scale


def halo(array, axis, dim, width):
    size, length = (lax.axis_size(axis), array.shape[dim])
    up = [(i, (i + 1) % size) for i in range(size)]
    down = [(j, i) for i, j in up]
    last = lax.slice_in_dim(array, length - width, length, axis=dim)
    first = lax.slice_in_dim(array, 0, width, axis=dim)
    before = lax.ppermute(last, axis, up)
    after = lax.ppermute(first, axis, down)
    return jnp.concatenate([before, array, after], axis=dim)


CHUNKS = 4


def cross_kernel(offs_ref, spec_ref, acc_ref, out_ref):
    segs, ext, width = spec_ref.shape
    half = width // 2
    start = R + offs_ref[pl.program_id(0)]
    rem = start % 8
    base = start - rem
    turn = (8 - rem) % 8
    keep = lax.broadcasted_iota(jnp.int32, (8, width), 0) < 8 - rem

    def body(r, carry):
        r0 = pl.multiple_of(R + r * 8, 8)
        p0 = pl.multiple_of(base + r * 8, 8)
        p1 = pl.multiple_of(jnp.minimum(p0 + 8, ext - 8), 8)
        o0 = pl.multiple_of(r * 8, 8)
        acc_m = acc_ref[pl.ds(o0, 8), 0:width]
        acc_lo = jnp.zeros((8, half), jnp.float32)
        acc_hi = acc_ref[pl.ds(o0, 8), width:]
        for s in range(segs):
            a = spec_ref[s, pl.ds(r0, 8), :]
            b0 = pltpu.roll(spec_ref[s, pl.ds(p0, 8), :], turn, 0)
            b1 = pltpu.roll(spec_ref[s, pl.ds(p1, 8), :], turn, 0)
            b = jnp.where(keep, b0, b1)
            acc_m = acc_m + a * b
            acc_lo = acc_lo + a[:, :half] * b[:, half:]
            acc_hi = acc_hi + a[:, half:] * b[:, :half]
        out_ref[pl.ds(o0, 8), 0:width] = acc_m
        out_ref[pl.ds(o0, 8), width:] = acc_hi - acc_lo
        return carry

    lax.fori_loop(0, (ext - 2 * R) // 8, body, 0, unroll=2)


def cross_spectra(spectra, offsets, acc):
    segs, ext, width = spectra.shape
    n_k, own_w, out_w = acc.shape
    grid_spec = pltpu.PrefetchScalarGridSpec(
        num_scalar_prefetch=1,
        grid=(n_k,),
        in_specs=[
            pl.BlockSpec(
                (segs, ext, width), lambda k, offs: (0, 0, 0), pipeline_mode=pl.Buffered(1)
            ),
            pl.BlockSpec((None, own_w, out_w), lambda k, offs: (k, 0, 0)),
        ],
        out_specs=pl.BlockSpec((None, own_w, out_w), lambda k, offs: (k, 0, 0)),
    )
    return pl.pallas_call(
        cross_kernel,
        grid_spec=grid_spec,
        out_shape=jax.ShapeDtypeStruct(acc.shape, jnp.float32),
        input_output_aliases={2: 0},
        compiler_params=pltpu.CompilerParams(
            dimension_semantics=("arbitrary",), vmem_limit_bytes=48 * 1024 * 1024
        ),
    )(offsets, spectra, acc)


def windows(piece, n_chan, width):
    segs, rows, channels = piece.shape
    blocks = piece.reshape(segs, rows, n_chan, channels // n_chan)
    before = jnp.roll(blocks, 1, axis=2)[..., -width:]
    after = jnp.roll(blocks, -1, axis=2)[..., :width]
    return jnp.concatenate([before, blocks, after], axis=3).transpose(2, 0, 1, 3)


def per_device(record, fir_taps, pair_offsets):
    n_chan = lax.axis_size("chan")
    n_time = lax.axis_size("tm")
    seg_count, part_rows, channels = record.shape
    block_width = channels // n_chan
    table = jnp.dot(fir_matrix_of(fir_taps, S), forward_table(S), precision=PRECISE)
    table = table.reshape(n_chan, part_rows, 2 * S)
    norm_scale = 1.0 / math.sqrt(seg_count * n_time * S)
    inverse = inverse_table(S, norm_scale)
    inverse_cat = jnp.concatenate([inverse[: 2 * S], inverse[2 * S :]], axis=0)
    even_offsets = pair_offsets[0::2]
    odd_offsets = pair_offsets[1::2]
    acc_shape = (even_offsets.shape[0], block_width, 3 * S)
    even = jnp.zeros(acc_shape, jnp.float32)
    odd = jnp.zeros(acc_shape, jnp.float32)
    step = seg_count // CHUNKS

    def exchange(g):
        piece = windows(lax.dynamic_slice_in_dim(record, g * step, step, 0), n_chan, R)
        return lax.all_to_all(piece, "chan", split_axis=0, concat_axis=0, tiled=True)

    def accumulate(turned, even, odd):
        spectra = jnp.einsum("asuc,auj->scj", turned, table, precision=FAST)
        return cross_spectra(spectra, even_offsets, even), cross_spectra(spectra, odd_offsets, odd)

    def body(g, carry):
        turned, even, odd = carry
        upcoming = exchange(g + 1)
        even, odd = accumulate(turned, even, odd)
        return upcoming, even, odd

    turned, even, odd = lax.fori_loop(0, CHUNKS - 1, body, (exchange(0), even, odd))
    even, odd = accumulate(turned, even, odd)

    def finish(crossed):
        lagged = jnp.einsum("kcr,rl->klc", crossed, inverse_cat, precision=FAST)
        parts = lax.all_to_all(lagged, "tm", split_axis=0, concat_axis=0, tiled=True)
        return jnp.sum(parts, axis=0, keepdims=True)

    first = finish(even)
    second = finish(odd)
    return jnp.concatenate([first, second], axis=0)


def solution(mesh):
    placed = (P("tm", "chan", None), P(), P())
    return jax.shard_map(
        per_device, mesh=mesh, in_specs=placed, out_specs=P("tm", None, "chan"), check_vma=False
    )
```

```python
import math

import jax
import jax.numpy as jnp
from jax import lax
from jax.experimental import pallas as pl
from jax.experimental.pallas import tpu as pltpu
from jax.sharding import PartitionSpec as P

S = 256
R = 128


PRECISE = lax.Precision.HIGHEST
FAST = lax.Precision.HIGH


def fir_matrix_of(fir_taps, seg_len):
    row_ids = lax.broadcasted_iota(jnp.int32, (seg_len, seg_len), 0)
    col_ids = lax.broadcasted_iota(jnp.int32, (seg_len, seg_len), 1)
    spread = col_ids - row_ids
    tap_ids = lax.broadcasted_iota(jnp.int32, (1, 1, fir_taps.shape[0]), 2)
    hits = spread[:, :, None] == tap_ids
    return jnp.sum(jnp.where(hits, fir_taps[None, None, :], 0.0), axis=2)


def forward_table(seg_len):
    length = 2 * seg_len
    time_ids = lax.broadcasted_iota(jnp.int32, (seg_len, length), 0)
    slot_ids = lax.broadcasted_iota(jnp.int32, (seg_len, length), 1)
    frequency = jnp.where(slot_ids <= seg_len, slot_ids, slot_ids - seg_len)
    angles = (frequency * time_ids % length).astype(jnp.float32) * (2.0 * math.pi / length)
    return jnp.where(slot_ids <= seg_len, jnp.cos(angles), jnp.sin(angles))


def inverse_table(seg_len, norm_scale):
    length = 2 * seg_len
    slot_ids = lax.broadcasted_iota(jnp.int32, (3 * seg_len, seg_len), 0)
    lag_ids = lax.broadcasted_iota(jnp.int32, (3 * seg_len, seg_len), 1) - seg_len // 2
    cosine_rows = slot_ids < length
    frequency = jnp.where(
        cosine_rows, jnp.where(slot_ids <= seg_len, slot_ids, slot_ids - seg_len), slot_ids - length
    )
    angles = (frequency * lag_ids % length).astype(jnp.float32) * (2.0 * math.pi / length)
    edge_rows = (slot_ids == 0) | (slot_ids == seg_len)
    cosine_weights = jnp.where(edge_rows, 1.0 / length, 2.0 / length)
    sine_weights = jnp.where(frequency == 0, 0.0, -2.0 / length)
    values = jnp.where(
        cosine_rows, cosine_weights * jnp.cos(angles), sine_weights * jnp.sin(angles)
    )
    return values * norm_scale


def halo(array, axis, dim, width):
    size, length = (lax.axis_size(axis), array.shape[dim])
    up = [(i, (i + 1) % size) for i in range(size)]
    down = [(j, i) for i, j in up]
    last = lax.slice_in_dim(array, length - width, length, axis=dim)
    first = lax.slice_in_dim(array, 0, width, axis=dim)
    before = lax.ppermute(last, axis, up)
    after = lax.ppermute(first, axis, down)
    return jnp.concatenate([before, array, after], axis=dim)


CHUNKS = 8


def cross_kernel(offs_ref, spec_ref, acc_ref, out_ref):
    segs, ext, width = spec_ref.shape
    half = width // 2
    start = R + offs_ref[pl.program_id(0)]
    rem = start % 8
    base = start - rem
    turn = (8 - rem) % 8
    keep = lax.broadcasted_iota(jnp.int32, (8, width), 0) < 8 - rem

    def body(r, carry):
        r0 = pl.multiple_of(R + r * 8, 8)
        p0 = pl.multiple_of(base + r * 8, 8)
        p1 = pl.multiple_of(jnp.minimum(p0 + 8, ext - 8), 8)
        o0 = pl.multiple_of(r * 8, 8)
        acc_m = acc_ref[pl.ds(o0, 8), 0:width]
        acc_lo = jnp.zeros((8, half), jnp.float32)
        acc_hi = acc_ref[pl.ds(o0, 8), width:]
        for s in range(segs):
            a = spec_ref[s, pl.ds(r0, 8), :]
            b0 = pltpu.roll(spec_ref[s, pl.ds(p0, 8), :], turn, 0)
            b1 = pltpu.roll(spec_ref[s, pl.ds(p1, 8), :], turn, 0)
            b = jnp.where(keep, b0, b1)
            acc_m = acc_m + a * b
            acc_lo = acc_lo + a[:, :half] * b[:, half:]
            acc_hi = acc_hi + a[:, half:] * b[:, :half]
        out_ref[pl.ds(o0, 8), 0:width] = acc_m
        out_ref[pl.ds(o0, 8), width:] = acc_hi - acc_lo
        return carry

    lax.fori_loop(0, (ext - 2 * R) // 8, body, 0, unroll=2)


def cross_spectra(spectra, offsets, acc):
    segs, ext, width = spectra.shape
    n_k, own_w, out_w = acc.shape
    grid_spec = pltpu.PrefetchScalarGridSpec(
        num_scalar_prefetch=1,
        grid=(n_k,),
        in_specs=[
            pl.BlockSpec(
                (segs, ext, width), lambda k, offs: (0, 0, 0), pipeline_mode=pl.Buffered(1)
            ),
            pl.BlockSpec((None, own_w, out_w), lambda k, offs: (k, 0, 0)),
        ],
        out_specs=pl.BlockSpec((None, own_w, out_w), lambda k, offs: (k, 0, 0)),
    )
    return pl.pallas_call(
        cross_kernel,
        grid_spec=grid_spec,
        out_shape=jax.ShapeDtypeStruct(acc.shape, jnp.float32),
        input_output_aliases={2: 0},
        compiler_params=pltpu.CompilerParams(
            dimension_semantics=("arbitrary",), vmem_limit_bytes=48 * 1024 * 1024
        ),
    )(offsets, spectra, acc)


def windows(piece, n_chan, width):
    segs, rows, channels = piece.shape
    blocks = piece.reshape(segs, rows, n_chan, channels // n_chan)
    before = jnp.roll(blocks, 1, axis=2)[..., -width:]
    after = jnp.roll(blocks, -1, axis=2)[..., :width]
    return jnp.concatenate([before, blocks, after], axis=3).transpose(2, 0, 1, 3)


def per_device(record, fir_taps, pair_offsets):
    n_chan = lax.axis_size("chan")
    n_time = lax.axis_size("tm")
    seg_count, part_rows, channels = record.shape
    block_width = channels // n_chan
    table = jnp.dot(fir_matrix_of(fir_taps, S), forward_table(S), precision=PRECISE)
    table = table.reshape(n_chan, part_rows, 2 * S)
    norm_scale = 1.0 / math.sqrt(seg_count * n_time * S)
    inverse = inverse_table(S, norm_scale)
    inverse_cat = jnp.concatenate([inverse[: 2 * S], inverse[2 * S :]], axis=0)
    even_offsets = pair_offsets[0::2]
    odd_offsets = pair_offsets[1::2]
    acc_shape = (even_offsets.shape[0], block_width, 3 * S)
    even = jnp.zeros(acc_shape, jnp.float32)
    odd = jnp.zeros(acc_shape, jnp.float32)
    step = seg_count // CHUNKS

    def exchange(g):
        piece = windows(lax.dynamic_slice_in_dim(record, g * step, step, 0), n_chan, R)
        return lax.all_to_all(piece, "chan", split_axis=0, concat_axis=0, tiled=True)

    def accumulate(turned, even, odd):
        spectra = jnp.einsum("asuc,auj->scj", turned, table, precision=FAST)
        return cross_spectra(spectra, even_offsets, even), cross_spectra(spectra, odd_offsets, odd)

    def body(g, carry):
        turned, even, odd = carry
        upcoming = exchange(g + 1)
        even, odd = accumulate(turned, even, odd)
        return upcoming, even, odd

    turned, even, odd = lax.fori_loop(0, CHUNKS - 1, body, (exchange(0), even, odd))
    even, odd = accumulate(turned, even, odd)

    def finish(crossed):
        lagged = jnp.einsum("kcr,rl->klc", crossed, inverse_cat, precision=FAST)
        parts = lax.all_to_all(lagged, "tm", split_axis=0, concat_axis=0, tiled=True)
        return jnp.sum(parts, axis=0, keepdims=True)

    first = finish(even)
    second = finish(odd)
    return jnp.concatenate([first, second], axis=0)


def solution(mesh):
    placed = (P("tm", "chan", None), P(), P())
    return jax.shard_map(
        per_device, mesh=mesh, in_specs=placed, out_specs=P("tm", None, "chan"), check_vma=False
    )
```

```python
import math

import jax
import jax.numpy as jnp
from jax import lax
from jax.experimental import pallas as pl
from jax.experimental.pallas import tpu as pltpu
from jax.sharding import PartitionSpec as P

S = 256
R = 128


PRECISE = lax.Precision.HIGHEST
FAST = lax.Precision.HIGH


def fir_matrix_of(fir_taps, seg_len):
    row_ids = lax.broadcasted_iota(jnp.int32, (seg_len, seg_len), 0)
    col_ids = lax.broadcasted_iota(jnp.int32, (seg_len, seg_len), 1)
    spread = col_ids - row_ids
    tap_ids = lax.broadcasted_iota(jnp.int32, (1, 1, fir_taps.shape[0]), 2)
    hits = spread[:, :, None] == tap_ids
    return jnp.sum(jnp.where(hits, fir_taps[None, None, :], 0.0), axis=2)


def forward_table(seg_len):
    length = 2 * seg_len
    time_ids = lax.broadcasted_iota(jnp.int32, (seg_len, length), 0)
    slot_ids = lax.broadcasted_iota(jnp.int32, (seg_len, length), 1)
    frequency = jnp.where(slot_ids <= seg_len, slot_ids, slot_ids - seg_len)
    angles = (frequency * time_ids % length).astype(jnp.float32) * (2.0 * math.pi / length)
    return jnp.where(slot_ids <= seg_len, jnp.cos(angles), jnp.sin(angles))


def inverse_table(seg_len, norm_scale):
    length = 2 * seg_len
    slot_ids = lax.broadcasted_iota(jnp.int32, (3 * seg_len, seg_len), 0)
    lag_ids = lax.broadcasted_iota(jnp.int32, (3 * seg_len, seg_len), 1) - seg_len // 2
    cosine_rows = slot_ids < length
    frequency = jnp.where(
        cosine_rows, jnp.where(slot_ids <= seg_len, slot_ids, slot_ids - seg_len), slot_ids - length
    )
    angles = (frequency * lag_ids % length).astype(jnp.float32) * (2.0 * math.pi / length)
    edge_rows = (slot_ids == 0) | (slot_ids == seg_len)
    cosine_weights = jnp.where(edge_rows, 1.0 / length, 2.0 / length)
    sine_weights = jnp.where(frequency == 0, 0.0, -2.0 / length)
    values = jnp.where(
        cosine_rows, cosine_weights * jnp.cos(angles), sine_weights * jnp.sin(angles)
    )
    return values * norm_scale


def halo(array, axis, dim, width):
    size, length = (lax.axis_size(axis), array.shape[dim])
    up = [(i, (i + 1) % size) for i in range(size)]
    down = [(j, i) for i, j in up]
    last = lax.slice_in_dim(array, length - width, length, axis=dim)
    first = lax.slice_in_dim(array, 0, width, axis=dim)
    before = lax.ppermute(last, axis, up)
    after = lax.ppermute(first, axis, down)
    return jnp.concatenate([before, array, after], axis=dim)


CHUNKS = 4


def cross_kernel(offs_ref, spec_ref, acc_ref, out_ref):
    segs, ext, width = spec_ref.shape
    half = width // 2
    start = R + offs_ref[pl.program_id(0)]
    rem = start % 8
    base = start - rem
    turn = (8 - rem) % 8
    keep = lax.broadcasted_iota(jnp.int32, (8, width), 0) < 8 - rem

    def body(r, carry):
        r0 = pl.multiple_of(R + r * 8, 8)
        p0 = pl.multiple_of(base + r * 8, 8)
        p1 = pl.multiple_of(jnp.minimum(p0 + 8, ext - 8), 8)
        o0 = pl.multiple_of(r * 8, 8)
        acc_m = acc_ref[pl.ds(o0, 8), 0:width]
        acc_lo = jnp.zeros((8, half), jnp.float32)
        acc_hi = acc_ref[pl.ds(o0, 8), width:]
        for s in range(segs):
            a = spec_ref[s, pl.ds(r0, 8), :]
            b0 = pltpu.roll(spec_ref[s, pl.ds(p0, 8), :], turn, 0)
            b1 = pltpu.roll(spec_ref[s, pl.ds(p1, 8), :], turn, 0)
            b = jnp.where(keep, b0, b1)
            acc_m = acc_m + a * b
            acc_lo = acc_lo + a[:, :half] * b[:, half:]
            acc_hi = acc_hi + a[:, half:] * b[:, :half]
        out_ref[pl.ds(o0, 8), 0:width] = acc_m
        out_ref[pl.ds(o0, 8), width:] = acc_hi - acc_lo
        return carry

    lax.fori_loop(0, (ext - 2 * R) // 8, body, 0, unroll=2)


def cross_spectra(spectra, offsets, acc):
    segs, ext, width = spectra.shape
    n_k, own_w, out_w = acc.shape
    grid_spec = pltpu.PrefetchScalarGridSpec(
        num_scalar_prefetch=1,
        grid=(n_k,),
        in_specs=[
            pl.BlockSpec(
                (segs, ext, width), lambda k, offs: (0, 0, 0), pipeline_mode=pl.Buffered(1)
            ),
            pl.BlockSpec((None, own_w, out_w), lambda k, offs: (k, 0, 0)),
        ],
        out_specs=pl.BlockSpec((None, own_w, out_w), lambda k, offs: (k, 0, 0)),
    )
    return pl.pallas_call(
        cross_kernel,
        grid_spec=grid_spec,
        out_shape=jax.ShapeDtypeStruct(acc.shape, jnp.float32),
        input_output_aliases={2: 0},
        compiler_params=pltpu.CompilerParams(
            dimension_semantics=("arbitrary",), vmem_limit_bytes=48 * 1024 * 1024
        ),
    )(offsets, spectra, acc)


def windows(piece, n_chan, width):
    segs, rows, channels = piece.shape
    blocks = piece.reshape(segs, rows, n_chan, channels // n_chan)
    before = jnp.roll(blocks, 1, axis=2)[..., -width:]
    after = jnp.roll(blocks, -1, axis=2)[..., :width]
    return jnp.concatenate([before, blocks, after], axis=3).transpose(2, 0, 1, 3)


def per_device(record, fir_taps, pair_offsets):
    n_chan = lax.axis_size("chan")
    n_time = lax.axis_size("tm")
    seg_count, part_rows, channels = record.shape
    block_width = channels // n_chan
    table = jnp.dot(fir_matrix_of(fir_taps, S), forward_table(S), precision=PRECISE)
    table = table.reshape(n_chan, part_rows, 2 * S)
    norm_scale = 1.0 / math.sqrt(seg_count * n_time * S)
    inverse = inverse_table(S, norm_scale)
    inverse_cat = jnp.concatenate([inverse[: 2 * S], inverse[2 * S :]], axis=0)
    even_offsets = pair_offsets[0::2]
    odd_offsets = pair_offsets[1::2]
    acc_shape = (even_offsets.shape[0], block_width, 3 * S)
    even = jnp.zeros(acc_shape, jnp.float32)
    odd = jnp.zeros(acc_shape, jnp.float32)
    step = seg_count // CHUNKS

    def exchange(g):
        piece = lax.dynamic_slice_in_dim(record, g * step, step, 0)
        piece = piece.reshape(step, part_rows, n_chan, block_width).transpose(2, 0, 1, 3)
        return lax.all_to_all(piece, "chan", split_axis=0, concat_axis=0, tiled=True)

    def accumulate(widened, even, odd):
        spectra = jnp.einsum("asuc,auj->scj", widened, table, precision=FAST)
        return cross_spectra(spectra, even_offsets, even), cross_spectra(spectra, odd_offsets, odd)

    def body(g, carry):
        turned, widened, even, odd = carry
        upcoming = exchange(g + 2)
        next_wide = halo(turned, "chan", 3, R)
        even, odd = accumulate(widened, even, odd)
        return upcoming, next_wide, even, odd

    first_wide = halo(exchange(0), "chan", 3, R)
    carry = (exchange(1), first_wide, even, odd)
    turned, widened, even, odd = lax.fori_loop(0, CHUNKS - 2, body, carry)
    last_wide = halo(turned, "chan", 3, R)
    even, odd = accumulate(widened, even, odd)
    even, odd = accumulate(last_wide, even, odd)

    def finish(crossed):
        lagged = jnp.einsum("kcr,rl->klc", crossed, inverse_cat, precision=FAST)
        parts = lax.all_to_all(lagged, "tm", split_axis=0, concat_axis=0, tiled=True)
        return jnp.sum(parts, axis=0, keepdims=True)

    first = finish(even)
    second = finish(odd)
    return jnp.concatenate([first, second], axis=0)


def solution(mesh):
    placed = (P("tm", "chan", None), P(), P())
    return jax.shard_map(
        per_device, mesh=mesh, in_specs=placed, out_specs=P("tm", None, "chan"), check_vma=False
    )
```

```python
import math

import jax
import jax.numpy as jnp
from jax import lax
from jax.experimental import pallas as pl
from jax.experimental.pallas import tpu as pltpu
from jax.sharding import PartitionSpec as P

S = 256
R = 128


PRECISE = lax.Precision.HIGHEST
FAST = lax.Precision.HIGH


def fir_matrix_of(fir_taps, seg_len):
    row_ids = lax.broadcasted_iota(jnp.int32, (seg_len, seg_len), 0)
    col_ids = lax.broadcasted_iota(jnp.int32, (seg_len, seg_len), 1)
    spread = col_ids - row_ids
    tap_ids = lax.broadcasted_iota(jnp.int32, (1, 1, fir_taps.shape[0]), 2)
    hits = spread[:, :, None] == tap_ids
    return jnp.sum(jnp.where(hits, fir_taps[None, None, :], 0.0), axis=2)


def forward_table(seg_len):
    length = 2 * seg_len
    time_ids = lax.broadcasted_iota(jnp.int32, (seg_len, length), 0)
    slot_ids = lax.broadcasted_iota(jnp.int32, (seg_len, length), 1)
    frequency = jnp.where(slot_ids <= seg_len, slot_ids, slot_ids - seg_len)
    angles = (frequency * time_ids % length).astype(jnp.float32) * (2.0 * math.pi / length)
    return jnp.where(slot_ids <= seg_len, jnp.cos(angles), jnp.sin(angles))


def inverse_table(seg_len, norm_scale):
    length = 2 * seg_len
    slot_ids = lax.broadcasted_iota(jnp.int32, (3 * seg_len, seg_len), 0)
    lag_ids = lax.broadcasted_iota(jnp.int32, (3 * seg_len, seg_len), 1) - seg_len // 2
    cosine_rows = slot_ids < length
    frequency = jnp.where(
        cosine_rows, jnp.where(slot_ids <= seg_len, slot_ids, slot_ids - seg_len), slot_ids - length
    )
    angles = (frequency * lag_ids % length).astype(jnp.float32) * (2.0 * math.pi / length)
    edge_rows = (slot_ids == 0) | (slot_ids == seg_len)
    cosine_weights = jnp.where(edge_rows, 1.0 / length, 2.0 / length)
    sine_weights = jnp.where(frequency == 0, 0.0, -2.0 / length)
    values = jnp.where(
        cosine_rows, cosine_weights * jnp.cos(angles), sine_weights * jnp.sin(angles)
    )
    return values * norm_scale


def halo(array, axis, dim, width):
    size, length = (lax.axis_size(axis), array.shape[dim])
    up = [(i, (i + 1) % size) for i in range(size)]
    down = [(j, i) for i, j in up]
    last = lax.slice_in_dim(array, length - width, length, axis=dim)
    first = lax.slice_in_dim(array, 0, width, axis=dim)
    before = lax.ppermute(last, axis, up)
    after = lax.ppermute(first, axis, down)
    return jnp.concatenate([before, array, after], axis=dim)


CHUNKS = 4


def cross_kernel(offs_ref, spec_ref, acc_ref, out_ref):
    segs, ext, width = spec_ref.shape
    half = width // 2
    start = R + offs_ref[pl.program_id(0)]
    rem = start % 8
    base = start - rem
    turn = (8 - rem) % 8
    keep = lax.broadcasted_iota(jnp.int32, (8, width), 0) < 8 - rem

    def body(r, carry):
        r0 = pl.multiple_of(R + r * 8, 8)
        p0 = pl.multiple_of(base + r * 8, 8)
        p1 = pl.multiple_of(jnp.minimum(p0 + 8, ext - 8), 8)
        o0 = pl.multiple_of(r * 8, 8)
        acc_m = acc_ref[pl.ds(o0, 8), 0:width]
        acc_lo = jnp.zeros((8, half), jnp.float32)
        acc_hi = acc_ref[pl.ds(o0, 8), width:]
        for s in range(segs):
            a = spec_ref[s, pl.ds(r0, 8), :]
            b0 = pltpu.roll(spec_ref[s, pl.ds(p0, 8), :], turn, 0)
            b1 = pltpu.roll(spec_ref[s, pl.ds(p1, 8), :], turn, 0)
            b = jnp.where(keep, b0, b1)
            acc_m = acc_m + a * b
            acc_lo = acc_lo + a[:, :half] * b[:, half:]
            acc_hi = acc_hi + a[:, half:] * b[:, :half]
        out_ref[pl.ds(o0, 8), 0:width] = acc_m
        out_ref[pl.ds(o0, 8), width:] = acc_hi - acc_lo
        return carry

    lax.fori_loop(0, (ext - 2 * R) // 8, body, 0, unroll=2)


def cross_spectra(spectra, offsets, acc):
    segs, ext, width = spectra.shape
    n_k, own_w, out_w = acc.shape
    grid_spec = pltpu.PrefetchScalarGridSpec(
        num_scalar_prefetch=1,
        grid=(n_k,),
        in_specs=[
            pl.BlockSpec(
                (segs, ext, width), lambda k, offs: (0, 0, 0), pipeline_mode=pl.Buffered(1)
            ),
            pl.BlockSpec((None, own_w, out_w), lambda k, offs: (k, 0, 0)),
        ],
        out_specs=pl.BlockSpec((None, own_w, out_w), lambda k, offs: (k, 0, 0)),
    )
    return pl.pallas_call(
        cross_kernel,
        grid_spec=grid_spec,
        out_shape=jax.ShapeDtypeStruct(acc.shape, jnp.float32),
        input_output_aliases={2: 0},
        compiler_params=pltpu.CompilerParams(
            dimension_semantics=("arbitrary",), vmem_limit_bytes=48 * 1024 * 1024
        ),
    )(offsets, spectra, acc)


def windows(piece, n_chan, width):
    segs, rows, channels = piece.shape
    blocks = piece.reshape(segs, rows, n_chan, channels // n_chan)
    before = jnp.roll(blocks, 1, axis=2)[..., -width:]
    after = jnp.roll(blocks, -1, axis=2)[..., :width]
    return jnp.concatenate([before, blocks, after], axis=3).transpose(2, 0, 1, 3)


def per_device(record, fir_taps, pair_offsets):
    n_chan = lax.axis_size("chan")
    n_time = lax.axis_size("tm")
    seg_count, part_rows, channels = record.shape
    block_width = channels // n_chan
    table = jnp.dot(fir_matrix_of(fir_taps, S), forward_table(S), precision=PRECISE)
    table = table.reshape(n_chan, part_rows, 2 * S)
    norm_scale = 1.0 / math.sqrt(seg_count * n_time * S)
    inverse = inverse_table(S, norm_scale)
    inverse_cat = jnp.concatenate([inverse[: 2 * S], inverse[2 * S :]], axis=0)
    even_offsets = pair_offsets[0::2]
    odd_offsets = pair_offsets[1::2]
    acc_shape = (even_offsets.shape[0], block_width, 3 * S)
    even = jnp.zeros(acc_shape, jnp.float32)
    odd = jnp.zeros(acc_shape, jnp.float32)
    step = seg_count // CHUNKS
    edge = step // 2

    def exchange(first, size):
        piece = windows(lax.dynamic_slice_in_dim(record, first, size, 0), n_chan, R)
        return lax.all_to_all(piece, "chan", split_axis=0, concat_axis=0, tiled=True)

    def accumulate(turned, even, odd):
        spectra = jnp.einsum("asuc,auj->scj", turned, table, precision=FAST)
        return cross_spectra(spectra, even_offsets, even), cross_spectra(spectra, odd_offsets, odd)

    def body(g, carry):
        turned, even, odd = carry
        upcoming = exchange(edge + (g + 1) * step, step)
        even, odd = accumulate(turned, even, odd)
        return upcoming, even, odd

    opening = exchange(0, edge)
    turned = exchange(edge, step)
    even, odd = accumulate(opening, even, odd)
    turned, even, odd = lax.fori_loop(0, CHUNKS - 2, body, (turned, even, odd))
    held, turned = lax.optimization_barrier((record, turned))
    piece = windows(lax.slice_in_dim(held, seg_count - edge, seg_count, axis=0), n_chan, R)
    closing = lax.all_to_all(piece, "chan", split_axis=0, concat_axis=0, tiled=True)
    even, odd = accumulate(turned, even, odd)
    even, odd = accumulate(closing, even, odd)

    def finish(crossed):
        lagged = jnp.einsum("kcr,rl->klc", crossed, inverse_cat, precision=FAST)
        parts = lax.all_to_all(lagged, "tm", split_axis=0, concat_axis=0, tiled=True)
        return jnp.sum(parts, axis=0, keepdims=True)

    first = finish(even)
    second = finish(odd)
    return jnp.concatenate([first, second], axis=0)


def solution(mesh):
    placed = (P("tm", "chan", None), P(), P())
    return jax.shard_map(
        per_device, mesh=mesh, in_specs=placed, out_specs=P("tm", None, "chan"), check_vma=False
    )
```

```python
import math

import jax
import jax.numpy as jnp
from jax import lax
from jax.experimental import pallas as pl
from jax.experimental.pallas import tpu as pltpu
from jax.sharding import PartitionSpec as P

S = 256
R = 128


PRECISE = lax.Precision.HIGHEST
FAST = lax.Precision.HIGH


def fir_matrix_of(fir_taps, seg_len):
    row_ids = lax.broadcasted_iota(jnp.int32, (seg_len, seg_len), 0)
    col_ids = lax.broadcasted_iota(jnp.int32, (seg_len, seg_len), 1)
    spread = col_ids - row_ids
    tap_ids = lax.broadcasted_iota(jnp.int32, (1, 1, fir_taps.shape[0]), 2)
    hits = spread[:, :, None] == tap_ids
    return jnp.sum(jnp.where(hits, fir_taps[None, None, :], 0.0), axis=2)


def forward_table(seg_len):
    length = 2 * seg_len
    time_ids = lax.broadcasted_iota(jnp.int32, (seg_len, length), 0)
    slot_ids = lax.broadcasted_iota(jnp.int32, (seg_len, length), 1)
    frequency = jnp.where(slot_ids <= seg_len, slot_ids, slot_ids - seg_len)
    angles = (frequency * time_ids % length).astype(jnp.float32) * (2.0 * math.pi / length)
    return jnp.where(slot_ids <= seg_len, jnp.cos(angles), jnp.sin(angles))


def inverse_table(seg_len, norm_scale):
    length = 2 * seg_len
    slot_ids = lax.broadcasted_iota(jnp.int32, (3 * seg_len, seg_len), 0)
    lag_ids = lax.broadcasted_iota(jnp.int32, (3 * seg_len, seg_len), 1) - seg_len // 2
    cosine_rows = slot_ids < length
    frequency = jnp.where(
        cosine_rows, jnp.where(slot_ids <= seg_len, slot_ids, slot_ids - seg_len), slot_ids - length
    )
    angles = (frequency * lag_ids % length).astype(jnp.float32) * (2.0 * math.pi / length)
    edge_rows = (slot_ids == 0) | (slot_ids == seg_len)
    cosine_weights = jnp.where(edge_rows, 1.0 / length, 2.0 / length)
    sine_weights = jnp.where(frequency == 0, 0.0, -2.0 / length)
    values = jnp.where(
        cosine_rows, cosine_weights * jnp.cos(angles), sine_weights * jnp.sin(angles)
    )
    return values * norm_scale


def halo(array, axis, dim, width):
    size, length = (lax.axis_size(axis), array.shape[dim])
    up = [(i, (i + 1) % size) for i in range(size)]
    down = [(j, i) for i, j in up]
    last = lax.slice_in_dim(array, length - width, length, axis=dim)
    first = lax.slice_in_dim(array, 0, width, axis=dim)
    before = lax.ppermute(last, axis, up)
    after = lax.ppermute(first, axis, down)
    return jnp.concatenate([before, array, after], axis=dim)


CHUNKS = 4


def cross_kernel(offs_ref, spec_ref, acc_ref, out_ref):
    segs, ext, width = spec_ref.shape
    half = width // 2
    start = R + offs_ref[pl.program_id(0)]
    rem = start % 8
    base = start - rem
    turn = (8 - rem) % 8
    keep = lax.broadcasted_iota(jnp.int32, (8, width), 0) < 8 - rem

    def body(r, carry):
        r0 = pl.multiple_of(R + r * 8, 8)
        p0 = pl.multiple_of(base + r * 8, 8)
        p1 = pl.multiple_of(jnp.minimum(p0 + 8, ext - 8), 8)
        o0 = pl.multiple_of(r * 8, 8)
        acc_m = acc_ref[pl.ds(o0, 8), 0:width]
        acc_lo = jnp.zeros((8, half), jnp.float32)
        acc_hi = acc_ref[pl.ds(o0, 8), width:]
        for s in range(segs):
            a = spec_ref[s, pl.ds(r0, 8), :]
            b0 = pltpu.roll(spec_ref[s, pl.ds(p0, 8), :], turn, 0)
            b1 = pltpu.roll(spec_ref[s, pl.ds(p1, 8), :], turn, 0)
            b = jnp.where(keep, b0, b1)
            acc_m = acc_m + a * b
            acc_lo = acc_lo + a[:, :half] * b[:, half:]
            acc_hi = acc_hi + a[:, half:] * b[:, :half]
        out_ref[pl.ds(o0, 8), 0:width] = acc_m
        out_ref[pl.ds(o0, 8), width:] = acc_hi - acc_lo
        return carry

    lax.fori_loop(0, (ext - 2 * R) // 8, body, 0, unroll=2)


def cross_spectra(spectra, offsets, acc):
    segs, ext, width = spectra.shape
    n_k, own_w, out_w = acc.shape
    grid_spec = pltpu.PrefetchScalarGridSpec(
        num_scalar_prefetch=1,
        grid=(n_k,),
        in_specs=[
            pl.BlockSpec(
                (segs, ext, width), lambda k, offs: (0, 0, 0), pipeline_mode=pl.Buffered(1)
            ),
            pl.BlockSpec((None, own_w, out_w), lambda k, offs: (k, 0, 0)),
        ],
        out_specs=pl.BlockSpec((None, own_w, out_w), lambda k, offs: (k, 0, 0)),
    )
    return pl.pallas_call(
        cross_kernel,
        grid_spec=grid_spec,
        out_shape=jax.ShapeDtypeStruct(acc.shape, jnp.float32),
        input_output_aliases={2: 0},
        compiler_params=pltpu.CompilerParams(
            dimension_semantics=("arbitrary",), vmem_limit_bytes=48 * 1024 * 1024
        ),
    )(offsets, spectra, acc)


def windows(piece, n_chan, width):
    segs, rows, channels = piece.shape
    blocks = piece.reshape(segs, rows, n_chan, channels // n_chan)
    before = jnp.roll(blocks, 1, axis=2)[..., -width:]
    after = jnp.roll(blocks, -1, axis=2)[..., :width]
    return jnp.concatenate([before, blocks, after], axis=3).transpose(2, 0, 1, 3)


def per_device(record, fir_taps, pair_offsets):
    n_chan = lax.axis_size("chan")
    n_time = lax.axis_size("tm")
    seg_count, part_rows, channels = record.shape
    block_width = channels // n_chan
    table = jnp.dot(fir_matrix_of(fir_taps, S), forward_table(S), precision=PRECISE)
    table = table.reshape(n_chan, part_rows, 2 * S)
    norm_scale = 1.0 / math.sqrt(seg_count * n_time * S)
    inverse = inverse_table(S, norm_scale)
    inverse_cat = jnp.concatenate([inverse[: 2 * S], inverse[2 * S :]], axis=0)
    even_offsets = pair_offsets[0::2]
    odd_offsets = pair_offsets[1::2]
    acc_shape = (even_offsets.shape[0], block_width, 3 * S)
    even = jnp.zeros(acc_shape, jnp.float32)
    odd = jnp.zeros(acc_shape, jnp.float32)
    step = seg_count // CHUNKS
    edge = step // 2

    def exchange(first, size):
        piece = windows(lax.dynamic_slice_in_dim(record, first, size, 0), n_chan, R)
        return lax.all_to_all(piece, "chan", split_axis=0, concat_axis=0, tiled=True)

    def accumulate(turned, even, odd):
        spectra = jnp.einsum("asuc,auj->scj", turned, table, precision=FAST)
        return cross_spectra(spectra, even_offsets, even), cross_spectra(spectra, odd_offsets, odd)

    def body(g, carry):
        turned, even, odd = carry
        upcoming = exchange(edge + (g + 1) * step, step)
        even, odd = accumulate(turned, even, odd)
        return upcoming, even, odd

    opening = exchange(0, edge)
    turned = exchange(edge, step)
    even, odd = accumulate(opening, even, odd)
    turned, even, odd = lax.fori_loop(0, CHUNKS - 2, body, (turned, even, odd))
    held, turned = lax.optimization_barrier((record, turned))
    piece = windows(lax.slice_in_dim(held, seg_count - edge, seg_count, axis=0), n_chan, R)
    closing = lax.all_to_all(piece, "chan", split_axis=0, concat_axis=0, tiled=True)
    even, odd = accumulate(turned, even, odd)
    closing, even, odd = lax.optimization_barrier((closing, even, odd))
    even, odd = accumulate(closing, even, odd)

    def finish(crossed):
        lagged = jnp.einsum("kcr,rl->kcl", crossed, inverse_cat, precision=FAST)
        parts = lax.all_to_all(lagged, "tm", split_axis=0, concat_axis=0, tiled=True)
        return jnp.sum(parts, axis=0, keepdims=True).transpose(0, 2, 1)

    first = finish(even)
    second = finish(odd)
    return jnp.concatenate([first, second], axis=0)


def solution(mesh):
    placed = (P("tm", "chan", None), P(), P())
    return jax.shard_map(
        per_device, mesh=mesh, in_specs=placed, out_specs=P("tm", None, "chan"), check_vma=False
    )
```

```python
import math

import jax
import jax.numpy as jnp
from jax import lax
from jax.experimental import pallas as pl
from jax.experimental.pallas import tpu as pltpu
from jax.sharding import PartitionSpec as P

S = 256
R = 128


PRECISE = lax.Precision.HIGHEST
FAST = lax.Precision.HIGH


def fir_matrix_of(fir_taps, seg_len):
    row_ids = lax.broadcasted_iota(jnp.int32, (seg_len, seg_len), 0)
    col_ids = lax.broadcasted_iota(jnp.int32, (seg_len, seg_len), 1)
    spread = col_ids - row_ids
    tap_ids = lax.broadcasted_iota(jnp.int32, (1, 1, fir_taps.shape[0]), 2)
    hits = spread[:, :, None] == tap_ids
    return jnp.sum(jnp.where(hits, fir_taps[None, None, :], 0.0), axis=2)


def forward_table(seg_len):
    length = 2 * seg_len
    time_ids = lax.broadcasted_iota(jnp.int32, (seg_len, length), 0)
    slot_ids = lax.broadcasted_iota(jnp.int32, (seg_len, length), 1)
    frequency = jnp.where(slot_ids <= seg_len, slot_ids, slot_ids - seg_len)
    angles = (frequency * time_ids % length).astype(jnp.float32) * (2.0 * math.pi / length)
    return jnp.where(slot_ids <= seg_len, jnp.cos(angles), jnp.sin(angles))


def inverse_table(seg_len, norm_scale):
    length = 2 * seg_len
    slot_ids = lax.broadcasted_iota(jnp.int32, (3 * seg_len, seg_len), 0)
    lag_ids = lax.broadcasted_iota(jnp.int32, (3 * seg_len, seg_len), 1) - seg_len // 2
    cosine_rows = slot_ids < length
    frequency = jnp.where(
        cosine_rows, jnp.where(slot_ids <= seg_len, slot_ids, slot_ids - seg_len), slot_ids - length
    )
    angles = (frequency * lag_ids % length).astype(jnp.float32) * (2.0 * math.pi / length)
    edge_rows = (slot_ids == 0) | (slot_ids == seg_len)
    cosine_weights = jnp.where(edge_rows, 1.0 / length, 2.0 / length)
    sine_weights = jnp.where(frequency == 0, 0.0, -2.0 / length)
    values = jnp.where(
        cosine_rows, cosine_weights * jnp.cos(angles), sine_weights * jnp.sin(angles)
    )
    return values * norm_scale


def halo(array, axis, dim, width):
    size, length = (lax.axis_size(axis), array.shape[dim])
    up = [(i, (i + 1) % size) for i in range(size)]
    down = [(j, i) for i, j in up]
    last = lax.slice_in_dim(array, length - width, length, axis=dim)
    first = lax.slice_in_dim(array, 0, width, axis=dim)
    before = lax.ppermute(last, axis, up)
    after = lax.ppermute(first, axis, down)
    return jnp.concatenate([before, array, after], axis=dim)


CHUNKS = 4


def cross_kernel(offs_ref, spec_ref, acc_ref, out_ref):
    segs, ext, width = spec_ref.shape
    half = width // 2
    start = R + offs_ref[pl.program_id(0)]
    rem = start % 8
    base = start - rem
    turn = (8 - rem) % 8
    keep = lax.broadcasted_iota(jnp.int32, (8, width), 0) < 8 - rem

    def body(r, carry):
        r0 = pl.multiple_of(R + r * 8, 8)
        p0 = pl.multiple_of(base + r * 8, 8)
        p1 = pl.multiple_of(jnp.minimum(p0 + 8, ext - 8), 8)
        o0 = pl.multiple_of(r * 8, 8)
        acc_m = acc_ref[pl.ds(o0, 8), 0:width]
        acc_lo = jnp.zeros((8, half), jnp.float32)
        acc_hi = acc_ref[pl.ds(o0, 8), width:]
        for s in range(segs):
            a = spec_ref[s, pl.ds(r0, 8), :]
            b0 = pltpu.roll(spec_ref[s, pl.ds(p0, 8), :], turn, 0)
            b1 = pltpu.roll(spec_ref[s, pl.ds(p1, 8), :], turn, 0)
            b = jnp.where(keep, b0, b1)
            acc_m = acc_m + a * b
            acc_lo = acc_lo + a[:, :half] * b[:, half:]
            acc_hi = acc_hi + a[:, half:] * b[:, :half]
        out_ref[pl.ds(o0, 8), 0:width] = acc_m
        out_ref[pl.ds(o0, 8), width:] = acc_hi - acc_lo
        return carry

    lax.fori_loop(0, (ext - 2 * R) // 8, body, 0, unroll=2)


def cross_spectra(spectra, offsets, acc):
    segs, ext, width = spectra.shape
    n_k, own_w, out_w = acc.shape
    grid_spec = pltpu.PrefetchScalarGridSpec(
        num_scalar_prefetch=1,
        grid=(n_k,),
        in_specs=[
            pl.BlockSpec(
                (segs, ext, width), lambda k, offs: (0, 0, 0), pipeline_mode=pl.Buffered(1)
            ),
            pl.BlockSpec((None, own_w, out_w), lambda k, offs: (k, 0, 0)),
        ],
        out_specs=pl.BlockSpec((None, own_w, out_w), lambda k, offs: (k, 0, 0)),
    )
    return pl.pallas_call(
        cross_kernel,
        grid_spec=grid_spec,
        out_shape=jax.ShapeDtypeStruct(acc.shape, jnp.float32),
        input_output_aliases={2: 0},
        compiler_params=pltpu.CompilerParams(
            dimension_semantics=("arbitrary",), vmem_limit_bytes=48 * 1024 * 1024
        ),
    )(offsets, spectra, acc)


def windows(piece, n_chan, width):
    segs, rows, channels = piece.shape
    blocks = piece.reshape(segs, rows, n_chan, channels // n_chan)
    before = jnp.roll(blocks, 1, axis=2)[..., -width:]
    after = jnp.roll(blocks, -1, axis=2)[..., :width]
    return jnp.concatenate([before, blocks, after], axis=3).transpose(2, 0, 1, 3)


def per_device(record, fir_taps, pair_offsets):
    n_chan = lax.axis_size("chan")
    n_time = lax.axis_size("tm")
    seg_count, part_rows, channels = record.shape
    block_width = channels // n_chan
    table = jnp.dot(fir_matrix_of(fir_taps, S), forward_table(S), precision=PRECISE)
    table = table.reshape(n_chan, part_rows, 2 * S)
    norm_scale = 1.0 / math.sqrt(seg_count * n_time * S)
    inverse = inverse_table(S, norm_scale)
    inverse_cat = jnp.concatenate([inverse[: 2 * S], inverse[2 * S :]], axis=0)
    even_offsets = pair_offsets[0::2]
    odd_offsets = pair_offsets[1::2]
    acc_shape = (even_offsets.shape[0], block_width, 3 * S)
    even = jnp.zeros(acc_shape, jnp.float32)
    odd = jnp.zeros(acc_shape, jnp.float32)
    step = seg_count // CHUNKS
    edge = step // 2

    def send(piece):
        return lax.all_to_all(piece, "chan", split_axis=0, concat_axis=0, tiled=True)

    def accumulate(turned, even, odd):
        spectra = jnp.einsum("asuc,auj->scj", turned, table, precision=FAST)
        return cross_spectra(spectra, even_offsets, even), cross_spectra(spectra, odd_offsets, odd)

    opening = send(windows(record[:edge], n_chan, R))
    rest = windows(record[edge:], n_chan, R)

    def body(g, carry):
        turned, even, odd = carry
        upcoming = send(lax.dynamic_slice_in_dim(rest, (g + 1) * step, step, 1))
        even, odd = accumulate(turned, even, odd)
        return upcoming, even, odd

    turned = send(rest[:, :step])
    even, odd = accumulate(opening, even, odd)
    turned, even, odd = lax.fori_loop(0, CHUNKS - 2, body, (turned, even, odd))
    held, turned = lax.optimization_barrier((rest, turned))
    closing = send(held[:, seg_count - 2 * edge :])
    even, odd = accumulate(turned, even, odd)
    even, odd = accumulate(closing, even, odd)

    def finish(crossed):
        lagged = jnp.einsum("kcr,rl->klc", crossed, inverse_cat, precision=FAST)
        parts = lax.all_to_all(lagged, "tm", split_axis=0, concat_axis=0, tiled=True)
        return jnp.sum(parts, axis=0, keepdims=True)

    first = finish(even)
    second = finish(odd)
    return jnp.concatenate([first, second], axis=0)


def solution(mesh):
    placed = (P("tm", "chan", None), P(), P())
    return jax.shard_map(
        per_device, mesh=mesh, in_specs=placed, out_specs=P("tm", None, "chan"), check_vma=False
    )
```

```python
import math

import jax
import jax.numpy as jnp
from jax import lax
from jax.experimental import pallas as pl
from jax.experimental.pallas import tpu as pltpu
from jax.sharding import PartitionSpec as P

S = 256
R = 128


PRECISE = lax.Precision.HIGHEST
FAST = lax.Precision.HIGH


def fir_matrix_of(fir_taps, seg_len):
    row_ids = lax.broadcasted_iota(jnp.int32, (seg_len, seg_len), 0)
    col_ids = lax.broadcasted_iota(jnp.int32, (seg_len, seg_len), 1)
    spread = col_ids - row_ids
    tap_ids = lax.broadcasted_iota(jnp.int32, (1, 1, fir_taps.shape[0]), 2)
    hits = spread[:, :, None] == tap_ids
    return jnp.sum(jnp.where(hits, fir_taps[None, None, :], 0.0), axis=2)


def forward_table(seg_len):
    length = 2 * seg_len
    time_ids = lax.broadcasted_iota(jnp.int32, (seg_len, length), 0)
    slot_ids = lax.broadcasted_iota(jnp.int32, (seg_len, length), 1)
    frequency = jnp.where(slot_ids <= seg_len, slot_ids, slot_ids - seg_len)
    angles = (frequency * time_ids % length).astype(jnp.float32) * (2.0 * math.pi / length)
    return jnp.where(slot_ids <= seg_len, jnp.cos(angles), jnp.sin(angles))


def inverse_table(seg_len, norm_scale):
    length = 2 * seg_len
    slot_ids = lax.broadcasted_iota(jnp.int32, (3 * seg_len, seg_len), 0)
    lag_ids = lax.broadcasted_iota(jnp.int32, (3 * seg_len, seg_len), 1) - seg_len // 2
    cosine_rows = slot_ids < length
    frequency = jnp.where(
        cosine_rows, jnp.where(slot_ids <= seg_len, slot_ids, slot_ids - seg_len), slot_ids - length
    )
    angles = (frequency * lag_ids % length).astype(jnp.float32) * (2.0 * math.pi / length)
    edge_rows = (slot_ids == 0) | (slot_ids == seg_len)
    cosine_weights = jnp.where(edge_rows, 1.0 / length, 2.0 / length)
    sine_weights = jnp.where(frequency == 0, 0.0, -2.0 / length)
    values = jnp.where(
        cosine_rows, cosine_weights * jnp.cos(angles), sine_weights * jnp.sin(angles)
    )
    return values * norm_scale


def halo(array, axis, dim, width):
    size, length = (lax.axis_size(axis), array.shape[dim])
    up = [(i, (i + 1) % size) for i in range(size)]
    down = [(j, i) for i, j in up]
    last = lax.slice_in_dim(array, length - width, length, axis=dim)
    first = lax.slice_in_dim(array, 0, width, axis=dim)
    before = lax.ppermute(last, axis, up)
    after = lax.ppermute(first, axis, down)
    return jnp.concatenate([before, array, after], axis=dim)


CHUNKS = 4


def cross_kernel(offs_ref, spec_ref, acc_ref, out_ref):
    segs, ext, width = spec_ref.shape
    half = width // 2
    start = R + offs_ref[pl.program_id(0)]
    rem = start % 8
    base = start - rem
    turn = (8 - rem) % 8
    keep = lax.broadcasted_iota(jnp.int32, (8, width), 0) < 8 - rem

    def body(r, carry):
        r0 = pl.multiple_of(R + r * 8, 8)
        p0 = pl.multiple_of(base + r * 8, 8)
        p1 = pl.multiple_of(jnp.minimum(p0 + 8, ext - 8), 8)
        o0 = pl.multiple_of(r * 8, 8)
        acc_m = acc_ref[pl.ds(o0, 8), 0:width]
        acc_lo = jnp.zeros((8, half), jnp.float32)
        acc_hi = acc_ref[pl.ds(o0, 8), width:]
        for s in range(segs):
            a = spec_ref[s, pl.ds(r0, 8), :]
            b0 = pltpu.roll(spec_ref[s, pl.ds(p0, 8), :], turn, 0)
            b1 = pltpu.roll(spec_ref[s, pl.ds(p1, 8), :], turn, 0)
            b = jnp.where(keep, b0, b1)
            acc_m = acc_m + a * b
            acc_lo = acc_lo + a[:, :half] * b[:, half:]
            acc_hi = acc_hi + a[:, half:] * b[:, :half]
        out_ref[pl.ds(o0, 8), 0:width] = acc_m
        out_ref[pl.ds(o0, 8), width:] = acc_hi - acc_lo
        return carry

    lax.fori_loop(0, (ext - 2 * R) // 8, body, 0, unroll=2)


def cross_spectra(spectra, offsets, acc):
    segs, ext, width = spectra.shape
    n_k, own_w, out_w = acc.shape
    grid_spec = pltpu.PrefetchScalarGridSpec(
        num_scalar_prefetch=1,
        grid=(n_k,),
        in_specs=[
            pl.BlockSpec(
                (segs, ext, width), lambda k, offs: (0, 0, 0), pipeline_mode=pl.Buffered(1)
            ),
            pl.BlockSpec((None, own_w, out_w), lambda k, offs: (k, 0, 0)),
        ],
        out_specs=pl.BlockSpec((None, own_w, out_w), lambda k, offs: (k, 0, 0)),
    )
    return pl.pallas_call(
        cross_kernel,
        grid_spec=grid_spec,
        out_shape=jax.ShapeDtypeStruct(acc.shape, jnp.float32),
        input_output_aliases={2: 0},
        compiler_params=pltpu.CompilerParams(
            dimension_semantics=("arbitrary",), vmem_limit_bytes=48 * 1024 * 1024
        ),
    )(offsets, spectra, acc)


def windows(piece, n_chan, width):
    segs, rows, channels = piece.shape
    blocks = piece.reshape(segs, rows, n_chan, channels // n_chan)
    before = jnp.roll(blocks, 1, axis=2)[..., -width:]
    after = jnp.roll(blocks, -1, axis=2)[..., :width]
    return jnp.concatenate([before, blocks, after], axis=3).transpose(2, 0, 1, 3)


def per_device(record, fir_taps, pair_offsets):
    n_chan = lax.axis_size("chan")
    n_time = lax.axis_size("tm")
    seg_count, part_rows, channels = record.shape
    block_width = channels // n_chan
    table = jnp.dot(fir_matrix_of(fir_taps, S), forward_table(S), precision=PRECISE)
    table = table.reshape(n_chan, part_rows, 2 * S)
    norm_scale = 1.0 / math.sqrt(seg_count * n_time * S)
    inverse = inverse_table(S, norm_scale)
    inverse_cat = jnp.concatenate([inverse[: 2 * S], inverse[2 * S :]], axis=0)
    even_offsets = pair_offsets[0::2]
    odd_offsets = pair_offsets[1::2]
    acc_shape = (even_offsets.shape[0], block_width, 3 * S)
    even = jnp.zeros(acc_shape, jnp.float32)
    odd = jnp.zeros(acc_shape, jnp.float32)
    step = seg_count // CHUNKS
    edge = step // 2

    def build(first, size):
        return windows(lax.dynamic_slice_in_dim(record, first, size, 0), n_chan, R)

    def send(piece):
        return lax.all_to_all(piece, "chan", split_axis=0, concat_axis=0, tiled=True)

    def accumulate(turned, even, odd):
        spectra = jnp.einsum("asuc,auj->scj", turned, table, precision=FAST)
        return cross_spectra(spectra, even_offsets, even), cross_spectra(spectra, odd_offsets, odd)

    def body(g, carry):
        turned, piece, even, odd = carry
        upcoming = send(piece)
        later = build(edge + (g + 2) * step, step)
        even, odd = accumulate(turned, even, odd)
        return upcoming, later, even, odd

    opening = send(build(0, edge))
    turned = send(build(edge, step))
    piece = build(edge + step, step)
    even, odd = accumulate(opening, even, odd)
    carry = (turned, piece, even, odd)
    turned, piece, even, odd = lax.fori_loop(0, CHUNKS - 2, body, carry)
    held, turned = lax.optimization_barrier((build(seg_count - edge, edge), turned))
    closing = send(held)
    even, odd = accumulate(turned, even, odd)
    even, odd = accumulate(closing, even, odd)

    def finish(crossed):
        lagged = jnp.einsum("kcr,rl->klc", crossed, inverse_cat, precision=FAST)
        parts = lax.all_to_all(lagged, "tm", split_axis=0, concat_axis=0, tiled=True)
        return jnp.sum(parts, axis=0, keepdims=True)

    first = finish(even)
    second = finish(odd)
    return jnp.concatenate([first, second], axis=0)


def solution(mesh):
    placed = (P("tm", "chan", None), P(), P())
    return jax.shard_map(
        per_device, mesh=mesh, in_specs=placed, out_specs=P("tm", None, "chan"), check_vma=False
    )
```

```python
import math

import jax
import jax.numpy as jnp
from jax import lax
from jax.experimental import pallas as pl
from jax.experimental.pallas import tpu as pltpu
from jax.sharding import PartitionSpec as P

S = 256
R = 128


PRECISE = lax.Precision.HIGHEST
FAST = lax.Precision.HIGH


def fir_matrix_of(fir_taps, seg_len):
    row_ids = lax.broadcasted_iota(jnp.int32, (seg_len, seg_len), 0)
    col_ids = lax.broadcasted_iota(jnp.int32, (seg_len, seg_len), 1)
    spread = col_ids - row_ids
    tap_ids = lax.broadcasted_iota(jnp.int32, (1, 1, fir_taps.shape[0]), 2)
    hits = spread[:, :, None] == tap_ids
    return jnp.sum(jnp.where(hits, fir_taps[None, None, :], 0.0), axis=2)


def forward_table(seg_len):
    length = 2 * seg_len
    time_ids = lax.broadcasted_iota(jnp.int32, (seg_len, length), 0)
    slot_ids = lax.broadcasted_iota(jnp.int32, (seg_len, length), 1)
    frequency = jnp.where(slot_ids <= seg_len, slot_ids, slot_ids - seg_len)
    angles = (frequency * time_ids % length).astype(jnp.float32) * (2.0 * math.pi / length)
    return jnp.where(slot_ids <= seg_len, jnp.cos(angles), jnp.sin(angles))


def inverse_table(seg_len, norm_scale):
    length = 2 * seg_len
    slot_ids = lax.broadcasted_iota(jnp.int32, (3 * seg_len, seg_len), 0)
    lag_ids = lax.broadcasted_iota(jnp.int32, (3 * seg_len, seg_len), 1) - seg_len // 2
    cosine_rows = slot_ids < length
    frequency = jnp.where(
        cosine_rows, jnp.where(slot_ids <= seg_len, slot_ids, slot_ids - seg_len), slot_ids - length
    )
    angles = (frequency * lag_ids % length).astype(jnp.float32) * (2.0 * math.pi / length)
    edge_rows = (slot_ids == 0) | (slot_ids == seg_len)
    cosine_weights = jnp.where(edge_rows, 1.0 / length, 2.0 / length)
    sine_weights = jnp.where(frequency == 0, 0.0, -2.0 / length)
    values = jnp.where(
        cosine_rows, cosine_weights * jnp.cos(angles), sine_weights * jnp.sin(angles)
    )
    return values * norm_scale


def halo(array, axis, dim, width):
    size, length = (lax.axis_size(axis), array.shape[dim])
    up = [(i, (i + 1) % size) for i in range(size)]
    down = [(j, i) for i, j in up]
    last = lax.slice_in_dim(array, length - width, length, axis=dim)
    first = lax.slice_in_dim(array, 0, width, axis=dim)
    before = lax.ppermute(last, axis, up)
    after = lax.ppermute(first, axis, down)
    return jnp.concatenate([before, array, after], axis=dim)


CHUNKS = 4


def cross_kernel(offs_ref, spec_ref, acc_ref, out_ref):
    segs, ext, width = spec_ref.shape
    half = width // 2
    start = R + offs_ref[pl.program_id(0)]
    rem = start % 8
    base = start - rem
    turn = (8 - rem) % 8
    keep = lax.broadcasted_iota(jnp.int32, (8, width), 0) < 8 - rem

    def body(r, carry):
        r0 = pl.multiple_of(R + r * 8, 8)
        p0 = pl.multiple_of(base + r * 8, 8)
        p1 = pl.multiple_of(jnp.minimum(p0 + 8, ext - 8), 8)
        o0 = pl.multiple_of(r * 8, 8)
        acc_m = acc_ref[pl.ds(o0, 8), 0:width]
        acc_lo = jnp.zeros((8, half), jnp.float32)
        acc_hi = acc_ref[pl.ds(o0, 8), width:]
        for s in range(segs):
            a = spec_ref[s, pl.ds(r0, 8), :]
            b0 = pltpu.roll(spec_ref[s, pl.ds(p0, 8), :], turn, 0)
            b1 = pltpu.roll(spec_ref[s, pl.ds(p1, 8), :], turn, 0)
            b = jnp.where(keep, b0, b1)
            acc_m = acc_m + a * b
            acc_lo = acc_lo + a[:, :half] * b[:, half:]
            acc_hi = acc_hi + a[:, half:] * b[:, :half]
        out_ref[pl.ds(o0, 8), 0:width] = acc_m
        out_ref[pl.ds(o0, 8), width:] = acc_hi - acc_lo
        return carry

    lax.fori_loop(0, (ext - 2 * R) // 8, body, 0, unroll=2)


def cross_spectra(spectra, offsets, acc):
    segs, ext, width = spectra.shape
    n_k, own_w, out_w = acc.shape
    grid_spec = pltpu.PrefetchScalarGridSpec(
        num_scalar_prefetch=1,
        grid=(n_k,),
        in_specs=[
            pl.BlockSpec(
                (segs, ext, width), lambda k, offs: (0, 0, 0), pipeline_mode=pl.Buffered(1)
            ),
            pl.BlockSpec((None, own_w, out_w), lambda k, offs: (k, 0, 0)),
        ],
        out_specs=pl.BlockSpec((None, own_w, out_w), lambda k, offs: (k, 0, 0)),
    )
    return pl.pallas_call(
        cross_kernel,
        grid_spec=grid_spec,
        out_shape=jax.ShapeDtypeStruct(acc.shape, jnp.float32),
        input_output_aliases={2: 0},
        compiler_params=pltpu.CompilerParams(
            dimension_semantics=("arbitrary",), vmem_limit_bytes=48 * 1024 * 1024
        ),
    )(offsets, spectra, acc)


def windows(piece, n_chan, width):
    segs, rows, channels = piece.shape
    blocks = piece.reshape(segs, rows, n_chan, channels // n_chan)
    before = jnp.roll(blocks, 1, axis=2)[..., -width:]
    after = jnp.roll(blocks, -1, axis=2)[..., :width]
    return jnp.concatenate([before, blocks, after], axis=3).transpose(2, 0, 1, 3)


def per_device(record, fir_taps, pair_offsets):
    n_chan = lax.axis_size("chan")
    n_time = lax.axis_size("tm")
    seg_count, part_rows, channels = record.shape
    block_width = channels // n_chan
    table = jnp.dot(fir_matrix_of(fir_taps, S), forward_table(S), precision=PRECISE)
    table = table.reshape(n_chan, part_rows, 2 * S)
    norm_scale = 1.0 / math.sqrt(seg_count * n_time * S)
    inverse = inverse_table(S, norm_scale)
    inverse_cat = jnp.concatenate([inverse[: 2 * S], inverse[2 * S :]], axis=0)
    ordered = jnp.concatenate([pair_offsets[0::2], pair_offsets[1::2]])
    half_k = pair_offsets.shape[0] // 2
    acc = jnp.zeros((pair_offsets.shape[0], block_width, 3 * S), jnp.float32)
    step = seg_count // CHUNKS
    edge = step // 2

    def build(first, size):
        return windows(lax.dynamic_slice_in_dim(record, first, size, 0), n_chan, R)

    def send(piece):
        return lax.all_to_all(piece, "chan", split_axis=0, concat_axis=0, tiled=True)

    def accumulate(turned, acc):
        spectra = jnp.einsum("asuc,auj->scj", turned, table, precision=FAST)
        return cross_spectra(spectra, ordered, acc)

    def body(g, carry):
        turned, piece, acc = carry
        upcoming = send(piece)
        later = build(edge + (g + 2) * step, step)
        acc = accumulate(turned, acc)
        return upcoming, later, acc

    opening = send(build(0, edge))
    turned = send(build(edge, step))
    piece = build(edge + step, step)
    acc = accumulate(opening, acc)
    turned, piece, acc = lax.fori_loop(0, CHUNKS - 2, body, (turned, piece, acc))
    held, turned = lax.optimization_barrier((build(seg_count - edge, edge), turned))
    closing = send(held)
    acc = accumulate(turned, acc)
    acc = accumulate(closing, acc)

    def finish(crossed):
        lagged = jnp.einsum("kcr,rl->klc", crossed, inverse_cat, precision=FAST)
        parts = lax.all_to_all(lagged, "tm", split_axis=0, concat_axis=0, tiled=True)
        return jnp.sum(parts, axis=0, keepdims=True)

    first = finish(acc[:half_k])
    second = finish(acc[half_k:])
    return jnp.concatenate([first, second], axis=0)


def solution(mesh):
    placed = (P("tm", "chan", None), P(), P())
    return jax.shard_map(
        per_device, mesh=mesh, in_specs=placed, out_specs=P("tm", None, "chan"), check_vma=False
    )
```

```python
import math

import jax
import jax.numpy as jnp
from jax import lax
from jax.experimental import pallas as pl
from jax.experimental.pallas import tpu as pltpu
from jax.sharding import PartitionSpec as P

S = 256
R = 128


PRECISE = lax.Precision.HIGHEST
FAST = lax.Precision.HIGH


def fir_matrix_of(fir_taps, seg_len):
    row_ids = lax.broadcasted_iota(jnp.int32, (seg_len, seg_len), 0)
    col_ids = lax.broadcasted_iota(jnp.int32, (seg_len, seg_len), 1)
    spread = col_ids - row_ids
    tap_ids = lax.broadcasted_iota(jnp.int32, (1, 1, fir_taps.shape[0]), 2)
    hits = spread[:, :, None] == tap_ids
    return jnp.sum(jnp.where(hits, fir_taps[None, None, :], 0.0), axis=2)


def forward_table(seg_len):
    length = 2 * seg_len
    time_ids = lax.broadcasted_iota(jnp.int32, (seg_len, length), 0)
    slot_ids = lax.broadcasted_iota(jnp.int32, (seg_len, length), 1)
    frequency = jnp.where(slot_ids <= seg_len, slot_ids, slot_ids - seg_len)
    angles = (frequency * time_ids % length).astype(jnp.float32) * (2.0 * math.pi / length)
    return jnp.where(slot_ids <= seg_len, jnp.cos(angles), jnp.sin(angles))


def inverse_table(seg_len, norm_scale):
    length = 2 * seg_len
    slot_ids = lax.broadcasted_iota(jnp.int32, (3 * seg_len, seg_len), 0)
    lag_ids = lax.broadcasted_iota(jnp.int32, (3 * seg_len, seg_len), 1) - seg_len // 2
    cosine_rows = slot_ids < length
    frequency = jnp.where(
        cosine_rows, jnp.where(slot_ids <= seg_len, slot_ids, slot_ids - seg_len), slot_ids - length
    )
    angles = (frequency * lag_ids % length).astype(jnp.float32) * (2.0 * math.pi / length)
    edge_rows = (slot_ids == 0) | (slot_ids == seg_len)
    cosine_weights = jnp.where(edge_rows, 1.0 / length, 2.0 / length)
    sine_weights = jnp.where(frequency == 0, 0.0, -2.0 / length)
    values = jnp.where(
        cosine_rows, cosine_weights * jnp.cos(angles), sine_weights * jnp.sin(angles)
    )
    return values * norm_scale


def halo(array, axis, dim, width):
    size, length = (lax.axis_size(axis), array.shape[dim])
    up = [(i, (i + 1) % size) for i in range(size)]
    down = [(j, i) for i, j in up]
    last = lax.slice_in_dim(array, length - width, length, axis=dim)
    first = lax.slice_in_dim(array, 0, width, axis=dim)
    before = lax.ppermute(last, axis, up)
    after = lax.ppermute(first, axis, down)
    return jnp.concatenate([before, array, after], axis=dim)


CHUNKS = 4


def cross_kernel(offs_ref, spec_ref, acc_ref, out_ref):
    segs, ext, width = spec_ref.shape
    half = width // 2
    start = R + offs_ref[pl.program_id(0)]
    rem = start % 8
    base = start - rem
    turn = (8 - rem) % 8
    keep = lax.broadcasted_iota(jnp.int32, (8, width), 0) < 8 - rem

    def body(r, carry):
        r0 = pl.multiple_of(R + r * 16, 8)
        p0 = pl.multiple_of(base + r * 16, 8)
        p2 = pl.multiple_of(jnp.minimum(p0 + 16, ext - 8), 8)
        o0 = pl.multiple_of(r * 16, 8)
        acc_m = [acc_ref[pl.ds(o0 + 8 * h, 8), 0:width] for h in range(2)]
        acc_hi = [acc_ref[pl.ds(o0 + 8 * h, 8), width:] for h in range(2)]
        acc_lo = [jnp.zeros((8, half), jnp.float32) for h in range(2)]
        for s in range(segs):
            c0 = pltpu.roll(spec_ref[s, pl.ds(p0, 8), :], turn, 0)
            c1 = pltpu.roll(spec_ref[s, pl.ds(p0 + 8, 8), :], turn, 0)
            c2 = pltpu.roll(spec_ref[s, pl.ds(p2, 8), :], turn, 0)
            partners = (jnp.where(keep, c0, c1), jnp.where(keep, c1, c2))
            for h in range(2):
                a = spec_ref[s, pl.ds(r0 + 8 * h, 8), :]
                b = partners[h]
                acc_m[h] = acc_m[h] + a * b
                acc_lo[h] = acc_lo[h] + a[:, :half] * b[:, half:]
                acc_hi[h] = acc_hi[h] + a[:, half:] * b[:, :half]
        for h in range(2):
            out_ref[pl.ds(o0 + 8 * h, 8), 0:width] = acc_m[h]
            out_ref[pl.ds(o0 + 8 * h, 8), width:] = acc_hi[h] - acc_lo[h]
        return carry

    lax.fori_loop(0, (ext - 2 * R) // 16, body, 0)


def cross_spectra(spectra, offsets, acc):
    segs, ext, width = spectra.shape
    n_k, own_w, out_w = acc.shape
    grid_spec = pltpu.PrefetchScalarGridSpec(
        num_scalar_prefetch=1,
        grid=(n_k,),
        in_specs=[
            pl.BlockSpec(
                (segs, ext, width), lambda k, offs: (0, 0, 0), pipeline_mode=pl.Buffered(1)
            ),
            pl.BlockSpec((None, own_w, out_w), lambda k, offs: (k, 0, 0)),
        ],
        out_specs=pl.BlockSpec((None, own_w, out_w), lambda k, offs: (k, 0, 0)),
    )
    return pl.pallas_call(
        cross_kernel,
        grid_spec=grid_spec,
        out_shape=jax.ShapeDtypeStruct(acc.shape, jnp.float32),
        input_output_aliases={2: 0},
        compiler_params=pltpu.CompilerParams(
            dimension_semantics=("arbitrary",), vmem_limit_bytes=48 * 1024 * 1024
        ),
    )(offsets, spectra, acc)


def windows(piece, n_chan, width):
    segs, rows, channels = piece.shape
    blocks = piece.reshape(segs, rows, n_chan, channels // n_chan)
    before = jnp.roll(blocks, 1, axis=2)[..., -width:]
    after = jnp.roll(blocks, -1, axis=2)[..., :width]
    return jnp.concatenate([before, blocks, after], axis=3).transpose(2, 0, 1, 3)


def per_device(record, fir_taps, pair_offsets):
    n_chan = lax.axis_size("chan")
    n_time = lax.axis_size("tm")
    seg_count, part_rows, channels = record.shape
    block_width = channels // n_chan
    table = jnp.dot(fir_matrix_of(fir_taps, S), forward_table(S), precision=PRECISE)
    table = table.reshape(n_chan, part_rows, 2 * S)
    norm_scale = 1.0 / math.sqrt(seg_count * n_time * S)
    inverse = inverse_table(S, norm_scale)
    inverse_cat = jnp.concatenate([inverse[: 2 * S], inverse[2 * S :]], axis=0)
    even_offsets = pair_offsets[0::2]
    odd_offsets = pair_offsets[1::2]
    acc_shape = (even_offsets.shape[0], block_width, 3 * S)
    even = jnp.zeros(acc_shape, jnp.float32)
    odd = jnp.zeros(acc_shape, jnp.float32)
    step = seg_count // CHUNKS
    edge = step // 2

    def build(first, size):
        return windows(lax.dynamic_slice_in_dim(record, first, size, 0), n_chan, R)

    def send(piece):
        return lax.all_to_all(piece, "chan", split_axis=0, concat_axis=0, tiled=True)

    def accumulate(turned, even, odd):
        spectra = jnp.einsum("asuc,auj->scj", turned, table, precision=FAST)
        return cross_spectra(spectra, even_offsets, even), cross_spectra(spectra, odd_offsets, odd)

    def body(g, carry):
        turned, piece, even, odd = carry
        upcoming = send(piece)
        later = build(edge + (g + 2) * step, step)
        even, odd = accumulate(turned, even, odd)
        return upcoming, later, even, odd

    opening = send(build(0, edge))
    turned = send(build(edge, step))
    piece = build(edge + step, step)
    even, odd = accumulate(opening, even, odd)
    carry = (turned, piece, even, odd)
    turned, piece, even, odd = lax.fori_loop(0, CHUNKS - 2, body, carry)
    held, turned = lax.optimization_barrier((build(seg_count - edge, edge), turned))
    closing = send(held)
    even, odd = accumulate(turned, even, odd)
    even, odd = accumulate(closing, even, odd)

    def finish(crossed):
        lagged = jnp.einsum("kcr,rl->klc", crossed, inverse_cat, precision=FAST)
        parts = lax.all_to_all(lagged, "tm", split_axis=0, concat_axis=0, tiled=True)
        return jnp.sum(parts, axis=0, keepdims=True)

    first = finish(even)
    second = finish(odd)
    return jnp.concatenate([first, second], axis=0)


def solution(mesh):
    placed = (P("tm", "chan", None), P(), P())
    return jax.shard_map(
        per_device, mesh=mesh, in_specs=placed, out_specs=P("tm", None, "chan"), check_vma=False
    )
```

```python
import math

import jax
import jax.numpy as jnp
from jax import lax
from jax.experimental import pallas as pl
from jax.experimental.pallas import tpu as pltpu
from jax.sharding import PartitionSpec as P

S = 256
R = 128


PRECISE = lax.Precision.HIGHEST
FAST = lax.Precision.HIGH


def fir_matrix_of(fir_taps, seg_len):
    row_ids = lax.broadcasted_iota(jnp.int32, (seg_len, seg_len), 0)
    col_ids = lax.broadcasted_iota(jnp.int32, (seg_len, seg_len), 1)
    spread = col_ids - row_ids
    tap_ids = lax.broadcasted_iota(jnp.int32, (1, 1, fir_taps.shape[0]), 2)
    hits = spread[:, :, None] == tap_ids
    return jnp.sum(jnp.where(hits, fir_taps[None, None, :], 0.0), axis=2)


def forward_table(seg_len):
    length = 2 * seg_len
    time_ids = lax.broadcasted_iota(jnp.int32, (seg_len, length), 0)
    slot_ids = lax.broadcasted_iota(jnp.int32, (seg_len, length), 1)
    frequency = jnp.where(slot_ids <= seg_len, slot_ids, slot_ids - seg_len)
    angles = (frequency * time_ids % length).astype(jnp.float32) * (2.0 * math.pi / length)
    return jnp.where(slot_ids <= seg_len, jnp.cos(angles), jnp.sin(angles))


def inverse_table(seg_len, norm_scale):
    length = 2 * seg_len
    slot_ids = lax.broadcasted_iota(jnp.int32, (3 * seg_len, seg_len), 0)
    lag_ids = lax.broadcasted_iota(jnp.int32, (3 * seg_len, seg_len), 1) - seg_len // 2
    cosine_rows = slot_ids < length
    frequency = jnp.where(
        cosine_rows, jnp.where(slot_ids <= seg_len, slot_ids, slot_ids - seg_len), slot_ids - length
    )
    angles = (frequency * lag_ids % length).astype(jnp.float32) * (2.0 * math.pi / length)
    edge_rows = (slot_ids == 0) | (slot_ids == seg_len)
    cosine_weights = jnp.where(edge_rows, 1.0 / length, 2.0 / length)
    sine_weights = jnp.where(frequency == 0, 0.0, -2.0 / length)
    values = jnp.where(
        cosine_rows, cosine_weights * jnp.cos(angles), sine_weights * jnp.sin(angles)
    )
    return values * norm_scale


def halo(array, axis, dim, width):
    size, length = (lax.axis_size(axis), array.shape[dim])
    up = [(i, (i + 1) % size) for i in range(size)]
    down = [(j, i) for i, j in up]
    last = lax.slice_in_dim(array, length - width, length, axis=dim)
    first = lax.slice_in_dim(array, 0, width, axis=dim)
    before = lax.ppermute(last, axis, up)
    after = lax.ppermute(first, axis, down)
    return jnp.concatenate([before, array, after], axis=dim)


CHUNKS = 4


def cross_kernel(offs_ref, *refs):
    spec_refs, acc_ref, out_ref = refs[:-2], refs[-2], refs[-1]
    ext, width = spec_refs[0].shape[1:]
    half = width // 2
    start = R + offs_ref[pl.program_id(0)]
    rem = start % 8
    base = start - rem
    turn = (8 - rem) % 8
    keep = lax.broadcasted_iota(jnp.int32, (8, width), 0) < 8 - rem

    def body(r, carry):
        r0 = pl.multiple_of(R + r * 16, 8)
        p0 = pl.multiple_of(base + r * 16, 8)
        p2 = pl.multiple_of(jnp.minimum(p0 + 16, ext - 8), 8)
        o0 = pl.multiple_of(r * 16, 8)
        acc_m = [acc_ref[pl.ds(o0 + 8 * h, 8), 0:width] for h in range(2)]
        acc_hi = [acc_ref[pl.ds(o0 + 8 * h, 8), width:] for h in range(2)]
        acc_lo = [jnp.zeros((8, half), jnp.float32) for h in range(2)]
        for spec_ref, s in [(f, s) for f in spec_refs for s in range(f.shape[0])]:
            c0 = pltpu.roll(spec_ref[s, pl.ds(p0, 8), :], turn, 0)
            c1 = pltpu.roll(spec_ref[s, pl.ds(p0 + 8, 8), :], turn, 0)
            c2 = pltpu.roll(spec_ref[s, pl.ds(p2, 8), :], turn, 0)
            partners = (jnp.where(keep, c0, c1), jnp.where(keep, c1, c2))
            for h in range(2):
                a = spec_ref[s, pl.ds(r0 + 8 * h, 8), :]
                b = partners[h]
                acc_m[h] = acc_m[h] + a * b
                acc_lo[h] = acc_lo[h] + a[:, :half] * b[:, half:]
                acc_hi[h] = acc_hi[h] + a[:, half:] * b[:, :half]
        for h in range(2):
            out_ref[pl.ds(o0 + 8 * h, 8), 0:width] = acc_m[h]
            out_ref[pl.ds(o0 + 8 * h, 8), width:] = acc_hi[h] - acc_lo[h]
        return carry

    lax.fori_loop(0, (ext - 2 * R) // 16, body, 0)


def cross_spectra(spectra_list, offsets, acc):
    n_k, own_w, out_w = acc.shape
    spec_specs = [
        pl.BlockSpec(f.shape, lambda k, offs: (0, 0, 0), pipeline_mode=pl.Buffered(1))
        for f in spectra_list
    ]
    grid_spec = pltpu.PrefetchScalarGridSpec(
        num_scalar_prefetch=1,
        grid=(n_k,),
        in_specs=spec_specs + [pl.BlockSpec((None, own_w, out_w), lambda k, offs: (k, 0, 0))],
        out_specs=pl.BlockSpec((None, own_w, out_w), lambda k, offs: (k, 0, 0)),
    )
    return pl.pallas_call(
        cross_kernel,
        grid_spec=grid_spec,
        out_shape=jax.ShapeDtypeStruct(acc.shape, jnp.float32),
        input_output_aliases={1 + len(spectra_list): 0},
        compiler_params=pltpu.CompilerParams(
            dimension_semantics=("arbitrary",), vmem_limit_bytes=48 * 1024 * 1024
        ),
    )(offsets, *spectra_list, acc)


def windows(piece, n_chan, width):
    segs, rows, channels = piece.shape
    blocks = piece.reshape(segs, rows, n_chan, channels // n_chan)
    before = jnp.roll(blocks, 1, axis=2)[..., -width:]
    after = jnp.roll(blocks, -1, axis=2)[..., :width]
    return jnp.concatenate([before, blocks, after], axis=3).transpose(2, 0, 1, 3)


def per_device(record, fir_taps, pair_offsets):
    n_chan = lax.axis_size("chan")
    n_time = lax.axis_size("tm")
    seg_count, part_rows, channels = record.shape
    block_width = channels // n_chan
    table = jnp.dot(fir_matrix_of(fir_taps, S), forward_table(S), precision=PRECISE)
    table = table.reshape(n_chan, part_rows, 2 * S)
    norm_scale = 1.0 / math.sqrt(seg_count * n_time * S)
    inverse = inverse_table(S, norm_scale)
    inverse_cat = jnp.concatenate([inverse[: 2 * S], inverse[2 * S :]], axis=0)
    even_offsets = pair_offsets[0::2]
    odd_offsets = pair_offsets[1::2]
    acc_shape = (even_offsets.shape[0], block_width, 3 * S)
    even = jnp.zeros(acc_shape, jnp.float32)
    odd = jnp.zeros(acc_shape, jnp.float32)
    step = seg_count // CHUNKS
    edge = step // 2

    def build(first, size):
        return windows(lax.dynamic_slice_in_dim(record, first, size, 0), n_chan, R)

    def send(piece):
        return lax.all_to_all(piece, "chan", split_axis=0, concat_axis=0, tiled=True)

    def spectra_of(turned):
        return jnp.einsum("asuc,auj->scj", turned, table, precision=FAST)

    def accumulate(turned, even, odd):
        spectra = [spectra_of(turned)]
        return cross_spectra(spectra, even_offsets, even), cross_spectra(spectra, odd_offsets, odd)

    def body(g, carry):
        turned, piece, even, odd = carry
        upcoming = send(piece)
        later = build(edge + (g + 2) * step, step)
        even, odd = accumulate(turned, even, odd)
        return upcoming, later, even, odd

    opening = send(build(0, edge))
    turned = send(build(edge, step))
    piece = build(edge + step, step)
    even, odd = accumulate(opening, even, odd)
    carry = (turned, piece, even, odd)
    turned, piece, even, odd = lax.fori_loop(0, CHUNKS - 2, body, carry)
    held, turned = lax.optimization_barrier((build(seg_count - edge, edge), turned))
    closing = send(held)
    last_full = spectra_of(turned)
    even = cross_spectra([last_full], even_offsets, even)
    last_small = spectra_of(closing)
    even = cross_spectra([last_small], even_offsets, even)
    odd = cross_spectra([last_full, last_small], odd_offsets, odd)

    def finish(crossed):
        lagged = jnp.einsum("kcr,rl->klc", crossed, inverse_cat, precision=FAST)
        parts = lax.all_to_all(lagged, "tm", split_axis=0, concat_axis=0, tiled=True)
        return jnp.sum(parts, axis=0, keepdims=True)

    first = finish(even)
    second = finish(odd)
    return jnp.concatenate([first, second], axis=0)


def solution(mesh):
    placed = (P("tm", "chan", None), P(), P())
    return jax.shard_map(
        per_device, mesh=mesh, in_specs=placed, out_specs=P("tm", None, "chan"), check_vma=False
    )
```

```python
import math

import jax
import jax.numpy as jnp
from jax import lax
from jax.experimental import pallas as pl
from jax.experimental.pallas import tpu as pltpu
from jax.sharding import PartitionSpec as P

S = 256
R = 128


PRECISE = lax.Precision.HIGHEST
FAST = lax.Precision.HIGH


def fir_matrix_of(fir_taps, seg_len):
    row_ids = lax.broadcasted_iota(jnp.int32, (seg_len, seg_len), 0)
    col_ids = lax.broadcasted_iota(jnp.int32, (seg_len, seg_len), 1)
    spread = col_ids - row_ids
    tap_ids = lax.broadcasted_iota(jnp.int32, (1, 1, fir_taps.shape[0]), 2)
    hits = spread[:, :, None] == tap_ids
    return jnp.sum(jnp.where(hits, fir_taps[None, None, :], 0.0), axis=2)


def forward_table(seg_len):
    length = 2 * seg_len
    time_ids = lax.broadcasted_iota(jnp.int32, (seg_len, length), 0)
    slot_ids = lax.broadcasted_iota(jnp.int32, (seg_len, length), 1)
    frequency = jnp.where(slot_ids <= seg_len, slot_ids, slot_ids - seg_len)
    angles = (frequency * time_ids % length).astype(jnp.float32) * (2.0 * math.pi / length)
    return jnp.where(slot_ids <= seg_len, jnp.cos(angles), jnp.sin(angles))


def inverse_table(seg_len, norm_scale):
    length = 2 * seg_len
    slot_ids = lax.broadcasted_iota(jnp.int32, (3 * seg_len, seg_len), 0)
    lag_ids = lax.broadcasted_iota(jnp.int32, (3 * seg_len, seg_len), 1) - seg_len // 2
    cosine_rows = slot_ids < length
    frequency = jnp.where(
        cosine_rows, jnp.where(slot_ids <= seg_len, slot_ids, slot_ids - seg_len), slot_ids - length
    )
    angles = (frequency * lag_ids % length).astype(jnp.float32) * (2.0 * math.pi / length)
    edge_rows = (slot_ids == 0) | (slot_ids == seg_len)
    cosine_weights = jnp.where(edge_rows, 1.0 / length, 2.0 / length)
    sine_weights = jnp.where(frequency == 0, 0.0, -2.0 / length)
    values = jnp.where(
        cosine_rows, cosine_weights * jnp.cos(angles), sine_weights * jnp.sin(angles)
    )
    return values * norm_scale


def halo(array, axis, dim, width):
    size, length = (lax.axis_size(axis), array.shape[dim])
    up = [(i, (i + 1) % size) for i in range(size)]
    down = [(j, i) for i, j in up]
    last = lax.slice_in_dim(array, length - width, length, axis=dim)
    first = lax.slice_in_dim(array, 0, width, axis=dim)
    before = lax.ppermute(last, axis, up)
    after = lax.ppermute(first, axis, down)
    return jnp.concatenate([before, array, after], axis=dim)


CHUNKS = 4


def cross_kernel(offs_ref, *refs):
    spec_refs, acc_ref, out_ref = refs[:-2], refs[-2], refs[-1]
    ext, width = spec_refs[0].shape[1:]
    half = width // 2
    start = R + offs_ref[pl.program_id(0)]
    rem = start % 8
    base = start - rem
    turn = (8 - rem) % 8
    keep = lax.broadcasted_iota(jnp.int32, (8, width), 0) < 8 - rem
    first = lax.broadcasted_iota(jnp.int32, (8, half), 1) == 0

    def body(r, carry):
        r0 = pl.multiple_of(R + r * 16, 8)
        p0 = pl.multiple_of(base + r * 16, 8)
        p2 = pl.multiple_of(jnp.minimum(p0 + 16, ext - 8), 8)
        o0 = pl.multiple_of(r * 16, 8)
        acc_m = [jnp.zeros((8, width), jnp.float32) for h in range(2)]
        acc_hi = [jnp.zeros((8, half), jnp.float32) for h in range(2)]
        acc_lo = [jnp.zeros((8, half), jnp.float32) for h in range(2)]
        for spec_ref, s in [(f, s) for f in spec_refs for s in range(f.shape[0])]:
            c0 = pltpu.roll(spec_ref[s, pl.ds(p0, 8), :], turn, 0)
            c1 = pltpu.roll(spec_ref[s, pl.ds(p0 + 8, 8), :], turn, 0)
            c2 = pltpu.roll(spec_ref[s, pl.ds(p2, 8), :], turn, 0)
            partners = (jnp.where(keep, c0, c1), jnp.where(keep, c1, c2))
            for h in range(2):
                a = spec_ref[s, pl.ds(r0 + 8 * h, 8), :]
                b = partners[h]
                acc_m[h] = acc_m[h] + a * b
                acc_lo[h] = acc_lo[h] + a[:, :half] * b[:, half:]
                acc_hi[h] = acc_hi[h] + a[:, half:] * b[:, :half]
        for h in range(2):
            rows = pl.ds(o0 + 8 * h, 8)
            cos_part = acc_m[h][:, :half]
            sin_part = acc_m[h][:, half:]
            skew = acc_hi[h] - acc_lo[h]
            out_ref[rows, 0:half] = acc_ref[rows, 0:half] + cos_part + jnp.where(first, 0.0, sin_part)
            out_ref[rows, half:] = acc_ref[rows, half:] + jnp.where(first, sin_part, skew)
        return carry

    lax.fori_loop(0, (ext - 2 * R) // 16, body, 0)


def cross_spectra(spectra_list, offsets, acc):
    n_k, own_w, out_w = acc.shape
    spec_specs = [
        pl.BlockSpec(f.shape, lambda k, offs: (0, 0, 0), pipeline_mode=pl.Buffered(1))
        for f in spectra_list
    ]
    grid_spec = pltpu.PrefetchScalarGridSpec(
        num_scalar_prefetch=1,
        grid=(n_k,),
        in_specs=spec_specs + [pl.BlockSpec((None, own_w, out_w), lambda k, offs: (k, 0, 0))],
        out_specs=pl.BlockSpec((None, own_w, out_w), lambda k, offs: (k, 0, 0)),
    )
    return pl.pallas_call(
        cross_kernel,
        grid_spec=grid_spec,
        out_shape=jax.ShapeDtypeStruct(acc.shape, jnp.float32),
        input_output_aliases={1 + len(spectra_list): 0},
        compiler_params=pltpu.CompilerParams(
            dimension_semantics=("arbitrary",), vmem_limit_bytes=48 * 1024 * 1024
        ),
    )(offsets, *spectra_list, acc)


def windows(piece, n_chan, width):
    segs, rows, channels = piece.shape
    blocks = piece.reshape(segs, rows, n_chan, channels // n_chan)
    before = jnp.roll(blocks, 1, axis=2)[..., -width:]
    after = jnp.roll(blocks, -1, axis=2)[..., :width]
    return jnp.concatenate([before, blocks, after], axis=3).transpose(2, 0, 1, 3)


def per_device(record, fir_taps, pair_offsets):
    n_chan = lax.axis_size("chan")
    n_time = lax.axis_size("tm")
    seg_count, part_rows, channels = record.shape
    block_width = channels // n_chan
    table = jnp.dot(fir_matrix_of(fir_taps, S), forward_table(S), precision=PRECISE)
    table = table.reshape(n_chan, part_rows, 2 * S)
    norm_scale = 1.0 / math.sqrt(seg_count * n_time * S)
    inverse = inverse_table(S, norm_scale)
    inverse_cat = jnp.concatenate([inverse[: S + 1], inverse[2 * S + 1 :]], axis=0)
    even_offsets = pair_offsets[0::2]
    odd_offsets = pair_offsets[1::2]
    acc_shape = (even_offsets.shape[0], block_width, 2 * S)
    even = jnp.zeros(acc_shape, jnp.float32)
    odd = jnp.zeros(acc_shape, jnp.float32)
    step = seg_count // CHUNKS
    edge = step // 2

    def build(first, size):
        return windows(lax.dynamic_slice_in_dim(record, first, size, 0), n_chan, R)

    def send(piece):
        return lax.all_to_all(piece, "chan", split_axis=0, concat_axis=0, tiled=True)

    def spectra_of(turned):
        return jnp.einsum("asuc,auj->scj", turned, table, precision=FAST)

    def accumulate(turned, even, odd):
        spectra = [spectra_of(turned)]
        return cross_spectra(spectra, even_offsets, even), cross_spectra(spectra, odd_offsets, odd)

    def body(g, carry):
        turned, piece, even, odd = carry
        upcoming = send(piece)
        later = build(edge + (g + 2) * step, step)
        even, odd = accumulate(turned, even, odd)
        return upcoming, later, even, odd

    opening = send(build(0, edge))
    turned = send(build(edge, step))
    piece = build(edge + step, step)
    even, odd = accumulate(opening, even, odd)
    carry = (turned, piece, even, odd)
    turned, piece, even, odd = lax.fori_loop(0, CHUNKS - 2, body, carry)
    held, turned = lax.optimization_barrier((build(seg_count - edge, edge), turned))
    closing = send(held)
    last_full = spectra_of(turned)
    even = cross_spectra([last_full], even_offsets, even)
    last_small = spectra_of(closing)
    even = cross_spectra([last_small], even_offsets, even)
    odd = cross_spectra([last_full, last_small], odd_offsets, odd)

    def finish(crossed):
        lagged = jnp.einsum("kcr,rl->klc", crossed, inverse_cat, precision=FAST)
        parts = lax.all_to_all(lagged, "tm", split_axis=0, concat_axis=0, tiled=True)
        return jnp.sum(parts, axis=0, keepdims=True)

    first = finish(even)
    second = finish(odd)
    return jnp.concatenate([first, second], axis=0)


def solution(mesh):
    placed = (P("tm", "chan", None), P(), P())
    return jax.shard_map(
        per_device, mesh=mesh, in_specs=placed, out_specs=P("tm", None, "chan"), check_vma=False
    )
```

```python
import math

import jax
import jax.numpy as jnp
from jax import lax
from jax.experimental import pallas as pl
from jax.experimental.pallas import tpu as pltpu
from jax.sharding import PartitionSpec as P

S = 256
R = 128


PRECISE = lax.Precision.HIGHEST
FAST = lax.Precision.HIGH


def fir_matrix_of(fir_taps, seg_len):
    row_ids = lax.broadcasted_iota(jnp.int32, (seg_len, seg_len), 0)
    col_ids = lax.broadcasted_iota(jnp.int32, (seg_len, seg_len), 1)
    spread = col_ids - row_ids
    tap_ids = lax.broadcasted_iota(jnp.int32, (1, 1, fir_taps.shape[0]), 2)
    hits = spread[:, :, None] == tap_ids
    return jnp.sum(jnp.where(hits, fir_taps[None, None, :], 0.0), axis=2)


def forward_table(seg_len):
    length = 2 * seg_len
    time_ids = lax.broadcasted_iota(jnp.int32, (seg_len, length), 0)
    slot_ids = lax.broadcasted_iota(jnp.int32, (seg_len, length), 1)
    frequency = jnp.where(slot_ids <= seg_len, slot_ids, slot_ids - seg_len)
    angles = (frequency * time_ids % length).astype(jnp.float32) * (2.0 * math.pi / length)
    return jnp.where(slot_ids <= seg_len, jnp.cos(angles), jnp.sin(angles))


def inverse_table(seg_len, norm_scale):
    length = 2 * seg_len
    slot_ids = lax.broadcasted_iota(jnp.int32, (3 * seg_len, seg_len), 0)
    lag_ids = lax.broadcasted_iota(jnp.int32, (3 * seg_len, seg_len), 1) - seg_len // 2
    cosine_rows = slot_ids < length
    frequency = jnp.where(
        cosine_rows, jnp.where(slot_ids <= seg_len, slot_ids, slot_ids - seg_len), slot_ids - length
    )
    angles = (frequency * lag_ids % length).astype(jnp.float32) * (2.0 * math.pi / length)
    edge_rows = (slot_ids == 0) | (slot_ids == seg_len)
    cosine_weights = jnp.where(edge_rows, 1.0 / length, 2.0 / length)
    sine_weights = jnp.where(frequency == 0, 0.0, -2.0 / length)
    values = jnp.where(
        cosine_rows, cosine_weights * jnp.cos(angles), sine_weights * jnp.sin(angles)
    )
    return values * norm_scale


def halo(array, axis, dim, width):
    size, length = (lax.axis_size(axis), array.shape[dim])
    up = [(i, (i + 1) % size) for i in range(size)]
    down = [(j, i) for i, j in up]
    last = lax.slice_in_dim(array, length - width, length, axis=dim)
    first = lax.slice_in_dim(array, 0, width, axis=dim)
    before = lax.ppermute(last, axis, up)
    after = lax.ppermute(first, axis, down)
    return jnp.concatenate([before, array, after], axis=dim)


CHUNKS = 4


def cross_kernel(offs_ref, *refs):
    spec_refs, acc_ref, out_ref = refs[:-2], refs[-2], refs[-1]
    ext, width = spec_refs[0].shape[1:]
    half = width // 2
    start = R + offs_ref[pl.program_id(0)]
    rem = start % 8
    base = start - rem
    turn = (8 - rem) % 8
    keep = lax.broadcasted_iota(jnp.int32, (8, width), 0) < 8 - rem
    first = lax.broadcasted_iota(jnp.int32, (8, half), 1) == 0

    def body(r, carry):
        r0 = pl.multiple_of(R + r * 16, 8)
        p0 = pl.multiple_of(base + r * 16, 8)
        p2 = pl.multiple_of(jnp.minimum(p0 + 16, ext - 8), 8)
        o0 = pl.multiple_of(r * 16, 8)
        acc_m = [jnp.zeros((8, width), jnp.float32) for h in range(2)]
        acc_hi = [jnp.zeros((8, half), jnp.float32) for h in range(2)]
        acc_lo = [jnp.zeros((8, half), jnp.float32) for h in range(2)]
        for spec_ref, s in [(f, s) for f in spec_refs for s in range(f.shape[0])]:
            c0 = pltpu.roll(spec_ref[s, pl.ds(p0, 8), :], turn, 0)
            c1 = pltpu.roll(spec_ref[s, pl.ds(p0 + 8, 8), :], turn, 0)
            c2 = pltpu.roll(spec_ref[s, pl.ds(p2, 8), :], turn, 0)
            partners = (jnp.where(keep, c0, c1), jnp.where(keep, c1, c2))
            for h in range(2):
                a = spec_ref[s, pl.ds(r0 + 8 * h, 8), :]
                b = partners[h]
                acc_m[h] = acc_m[h] + a * b
                acc_lo[h] = acc_lo[h] + a[:, :half] * b[:, half:]
                acc_hi[h] = acc_hi[h] + a[:, half:] * b[:, :half]
        for h in range(2):
            rows = pl.ds(o0 + 8 * h, 8)
            cos_part = acc_m[h][:, :half]
            sin_part = acc_m[h][:, half:]
            skew = acc_hi[h] - acc_lo[h]
            out_ref[rows, 0:half] = acc_ref[rows, 0:half] + cos_part + jnp.where(first, 0.0, sin_part)
            out_ref[rows, half:] = acc_ref[rows, half:] + jnp.where(first, sin_part, skew)
        return carry

    lax.fori_loop(0, (ext - 2 * R) // 16, body, 0)


def cross_spectra(spectra_list, offsets, acc):
    n_k, own_w, out_w = acc.shape
    spec_specs = [
        pl.BlockSpec(f.shape, lambda k, offs: (0, 0, 0), pipeline_mode=pl.Buffered(1))
        for f in spectra_list
    ]
    grid_spec = pltpu.PrefetchScalarGridSpec(
        num_scalar_prefetch=1,
        grid=(n_k,),
        in_specs=spec_specs + [pl.BlockSpec((None, own_w, out_w), lambda k, offs: (k, 0, 0))],
        out_specs=pl.BlockSpec((None, own_w, out_w), lambda k, offs: (k, 0, 0)),
    )
    return pl.pallas_call(
        cross_kernel,
        grid_spec=grid_spec,
        out_shape=jax.ShapeDtypeStruct(acc.shape, jnp.float32),
        input_output_aliases={1 + len(spectra_list): 0},
        compiler_params=pltpu.CompilerParams(
            dimension_semantics=("arbitrary",), vmem_limit_bytes=48 * 1024 * 1024
        ),
    )(offsets, *spectra_list, acc)


def windows(piece, n_chan, width):
    segs, rows, channels = piece.shape
    blocks = piece.reshape(segs, rows, n_chan, channels // n_chan)
    before = jnp.roll(blocks, 1, axis=2)[..., -width:]
    after = jnp.roll(blocks, -1, axis=2)[..., :width]
    return jnp.concatenate([before, blocks, after], axis=3).transpose(2, 0, 1, 3)


def per_device(record, fir_taps, pair_offsets):
    n_chan = lax.axis_size("chan")
    n_time = lax.axis_size("tm")
    seg_count, part_rows, channels = record.shape
    block_width = channels // n_chan
    table = jnp.dot(fir_matrix_of(fir_taps, S), forward_table(S), precision=PRECISE)
    table = table.reshape(n_chan, part_rows, 2 * S)
    norm_scale = 1.0 / math.sqrt(seg_count * n_time * S)
    inverse = inverse_table(S, norm_scale)
    inverse_cat = jnp.concatenate([inverse[: S + 1], inverse[2 * S + 1 :]], axis=0)
    even_offsets = pair_offsets[0::2]
    odd_offsets = pair_offsets[1::2]
    acc_shape = (even_offsets.shape[0], block_width, 2 * S)
    even = jnp.zeros(acc_shape, jnp.float32)
    odd = jnp.zeros(acc_shape, jnp.float32)
    step = seg_count // CHUNKS
    edge = step // 2

    def build(first, size):
        return windows(lax.dynamic_slice_in_dim(record, first, size, 0), n_chan, R)

    def send(piece):
        return lax.all_to_all(piece, "chan", split_axis=0, concat_axis=0, tiled=True)

    def spectra_of(turned):
        return jnp.einsum("asuc,auj->scj", turned, table, precision=FAST)

    def accumulate(turned, even, odd):
        spectra = [spectra_of(turned)]
        return cross_spectra(spectra, even_offsets, even), cross_spectra(spectra, odd_offsets, odd)

    def body(g, carry):
        turned, piece, even, odd = carry
        upcoming = send(piece)
        later = build(edge + (g + 2) * step, step)
        even, odd = accumulate(turned, even, odd)
        return upcoming, later, even, odd

    opening = send(build(0, edge))
    turned = send(build(edge, step))
    piece = build(edge + step, step)
    even, odd = accumulate(opening, even, odd)
    carry = (turned, piece, even, odd)
    turned, piece, even, odd = lax.fori_loop(0, CHUNKS - 2, body, carry)
    held, turned = lax.optimization_barrier((build(seg_count - edge, edge), turned))
    closing = send(held)
    last_full = spectra_of(turned)
    even = cross_spectra([last_full], even_offsets, even)
    last_small = spectra_of(closing)
    even = cross_spectra([last_small], even_offsets, even)
    odd = cross_spectra([last_full, last_small], odd_offsets, odd)

    def finish(crossed, offload):
        lagged = jnp.einsum("kcr,rl->klc", crossed, inverse_cat, precision=FAST)
        if offload:
            return lax.psum_scatter(lagged, "tm", scatter_dimension=0, tiled=True)
        parts = lax.all_to_all(lagged, "tm", split_axis=0, concat_axis=0, tiled=True)
        return jnp.sum(parts, axis=0, keepdims=True)

    first = finish(even, True)
    second = finish(odd, False)
    return jnp.concatenate([first, second], axis=0)


def solution(mesh):
    placed = (P("tm", "chan", None), P(), P())
    return jax.shard_map(
        per_device, mesh=mesh, in_specs=placed, out_specs=P("tm", None, "chan"), check_vma=False
    )
```

```python
import math

import jax
import jax.numpy as jnp
from jax import lax
from jax.experimental import pallas as pl
from jax.experimental.pallas import tpu as pltpu
from jax.sharding import PartitionSpec as P

S = 256
R = 128


PRECISE = lax.Precision.HIGHEST
FAST = lax.Precision.HIGH


def fir_matrix_of(fir_taps, seg_len):
    row_ids = lax.broadcasted_iota(jnp.int32, (seg_len, seg_len), 0)
    col_ids = lax.broadcasted_iota(jnp.int32, (seg_len, seg_len), 1)
    spread = col_ids - row_ids
    tap_ids = lax.broadcasted_iota(jnp.int32, (1, 1, fir_taps.shape[0]), 2)
    hits = spread[:, :, None] == tap_ids
    return jnp.sum(jnp.where(hits, fir_taps[None, None, :], 0.0), axis=2)


def forward_table(seg_len):
    length = 2 * seg_len
    time_ids = lax.broadcasted_iota(jnp.int32, (seg_len, length), 0)
    slot_ids = lax.broadcasted_iota(jnp.int32, (seg_len, length), 1)
    frequency = jnp.where(slot_ids <= seg_len, slot_ids, slot_ids - seg_len)
    angles = (frequency * time_ids % length).astype(jnp.float32) * (2.0 * math.pi / length)
    return jnp.where(slot_ids <= seg_len, jnp.cos(angles), jnp.sin(angles))


def inverse_table(seg_len, norm_scale):
    length = 2 * seg_len
    slot_ids = lax.broadcasted_iota(jnp.int32, (3 * seg_len, seg_len), 0)
    lag_ids = lax.broadcasted_iota(jnp.int32, (3 * seg_len, seg_len), 1) - seg_len // 2
    cosine_rows = slot_ids < length
    frequency = jnp.where(
        cosine_rows, jnp.where(slot_ids <= seg_len, slot_ids, slot_ids - seg_len), slot_ids - length
    )
    angles = (frequency * lag_ids % length).astype(jnp.float32) * (2.0 * math.pi / length)
    edge_rows = (slot_ids == 0) | (slot_ids == seg_len)
    cosine_weights = jnp.where(edge_rows, 1.0 / length, 2.0 / length)
    sine_weights = jnp.where(frequency == 0, 0.0, -2.0 / length)
    values = jnp.where(
        cosine_rows, cosine_weights * jnp.cos(angles), sine_weights * jnp.sin(angles)
    )
    return values * norm_scale


def halo(array, axis, dim, width):
    size, length = (lax.axis_size(axis), array.shape[dim])
    up = [(i, (i + 1) % size) for i in range(size)]
    down = [(j, i) for i, j in up]
    last = lax.slice_in_dim(array, length - width, length, axis=dim)
    first = lax.slice_in_dim(array, 0, width, axis=dim)
    before = lax.ppermute(last, axis, up)
    after = lax.ppermute(first, axis, down)
    return jnp.concatenate([before, array, after], axis=dim)


CHUNKS = 4


def cross_kernel(offs_ref, *refs):
    spec_refs, acc_ref, out_ref = refs[:-2], refs[-2], refs[-1]
    ext, width = spec_refs[0].shape[1:]
    half = width // 2
    start = R + offs_ref[pl.program_id(0)]
    rem = start % 8
    base = start - rem
    turn = (8 - rem) % 8
    keep = lax.broadcasted_iota(jnp.int32, (8, width), 0) < 8 - rem
    first = lax.broadcasted_iota(jnp.int32, (8, half), 1) == 0

    def body(r, carry):
        r0 = pl.multiple_of(R + r * 16, 8)
        p0 = pl.multiple_of(base + r * 16, 8)
        p2 = pl.multiple_of(jnp.minimum(p0 + 16, ext - 8), 8)
        o0 = pl.multiple_of(r * 16, 8)
        acc_m = [jnp.zeros((8, width), jnp.float32) for h in range(2)]
        acc_hi = [jnp.zeros((8, half), jnp.float32) for h in range(2)]
        acc_lo = [jnp.zeros((8, half), jnp.float32) for h in range(2)]
        for spec_ref, s in [(f, s) for f in spec_refs for s in range(f.shape[0])]:
            c0 = pltpu.roll(spec_ref[s, pl.ds(p0, 8), :], turn, 0)
            c1 = pltpu.roll(spec_ref[s, pl.ds(p0 + 8, 8), :], turn, 0)
            c2 = pltpu.roll(spec_ref[s, pl.ds(p2, 8), :], turn, 0)
            partners = (jnp.where(keep, c0, c1), jnp.where(keep, c1, c2))
            for h in range(2):
                a = spec_ref[s, pl.ds(r0 + 8 * h, 8), :]
                b = partners[h]
                acc_m[h] = acc_m[h] + a * b
                acc_lo[h] = acc_lo[h] + a[:, :half] * b[:, half:]
                acc_hi[h] = acc_hi[h] + a[:, half:] * b[:, :half]
        for h in range(2):
            rows = pl.ds(o0 + 8 * h, 8)
            cos_part = acc_m[h][:, :half]
            sin_part = acc_m[h][:, half:]
            skew = acc_hi[h] - acc_lo[h]
            out_ref[rows, 0:half] = acc_ref[rows, 0:half] + cos_part + jnp.where(first, 0.0, sin_part)
            out_ref[rows, half:] = acc_ref[rows, half:] + jnp.where(first, sin_part, skew)
        return carry

    lax.fori_loop(0, (ext - 2 * R) // 16, body, 0)


def cross_spectra(spectra_list, offsets, acc):
    n_k, own_w, out_w = acc.shape
    spec_specs = [
        pl.BlockSpec(f.shape, lambda k, offs: (0, 0, 0), pipeline_mode=pl.Buffered(1))
        for f in spectra_list
    ]
    grid_spec = pltpu.PrefetchScalarGridSpec(
        num_scalar_prefetch=1,
        grid=(n_k,),
        in_specs=spec_specs + [pl.BlockSpec((None, own_w, out_w), lambda k, offs: (k, 0, 0))],
        out_specs=pl.BlockSpec((None, own_w, out_w), lambda k, offs: (k, 0, 0)),
    )
    return pl.pallas_call(
        cross_kernel,
        grid_spec=grid_spec,
        out_shape=jax.ShapeDtypeStruct(acc.shape, jnp.float32),
        input_output_aliases={1 + len(spectra_list): 0},
        compiler_params=pltpu.CompilerParams(
            dimension_semantics=("arbitrary",), vmem_limit_bytes=48 * 1024 * 1024
        ),
    )(offsets, *spectra_list, acc)


def windows(piece, n_chan, width):
    segs, rows, channels = piece.shape
    blocks = piece.reshape(segs, rows, n_chan, channels // n_chan)
    before = jnp.roll(blocks, 1, axis=2)[..., -width:]
    after = jnp.roll(blocks, -1, axis=2)[..., :width]
    return jnp.concatenate([before, blocks, after], axis=3).transpose(2, 0, 1, 3)


def per_device(record, fir_taps, pair_offsets):
    n_chan = lax.axis_size("chan")
    n_time = lax.axis_size("tm")
    seg_count, part_rows, channels = record.shape
    block_width = channels // n_chan
    table = jnp.dot(fir_matrix_of(fir_taps, S), forward_table(S), precision=PRECISE)
    table = table.reshape(n_chan, part_rows, 2 * S)
    norm_scale = 1.0 / math.sqrt(seg_count * n_time * S)
    inverse = inverse_table(S, norm_scale)
    inverse_cat = jnp.concatenate([inverse[: S + 1], inverse[2 * S + 1 :]], axis=0)
    even_offsets = pair_offsets[0::2]
    odd_offsets = pair_offsets[1::2]
    acc_shape = (even_offsets.shape[0], block_width, 2 * S)
    even = jnp.zeros(acc_shape, jnp.float32)
    odd = jnp.zeros(acc_shape, jnp.float32)
    step = seg_count // CHUNKS
    edge = step // 2

    def build(first, size):
        return windows(lax.dynamic_slice_in_dim(record, first, size, 0), n_chan, R)

    def send(piece):
        return lax.all_to_all(piece, "chan", split_axis=0, concat_axis=0, tiled=True)

    def spectra_of(turned):
        return jnp.einsum("asuc,auj->scj", turned, table, precision=FAST)

    def accumulate(turned, even, odd):
        spectra = [spectra_of(turned)]
        return cross_spectra(spectra, even_offsets, even), cross_spectra(spectra, odd_offsets, odd)

    def body(g, carry):
        turned, piece, even, odd = carry
        upcoming = send(piece)
        later = build(edge + (g + 2) * step, step)
        even, odd = accumulate(turned, even, odd)
        return upcoming, later, even, odd

    opening = send(build(0, edge))
    record_later, opening = lax.optimization_barrier((record, opening))
    turned = send(windows(record_later[edge : edge + step], n_chan, R))
    piece = windows(record_later[edge + step : edge + 2 * step], n_chan, R)
    even, odd = accumulate(opening, even, odd)
    carry = (turned, piece, even, odd)
    turned, piece, even, odd = lax.fori_loop(0, CHUNKS - 2, body, carry)
    held, turned = lax.optimization_barrier((build(seg_count - edge, edge), turned))
    closing = send(held)
    last_full = spectra_of(turned)
    even = cross_spectra([last_full], even_offsets, even)
    last_small = spectra_of(closing)
    even = cross_spectra([last_small], even_offsets, even)
    odd = cross_spectra([last_full, last_small], odd_offsets, odd)

    def finish(crossed):
        lagged = jnp.einsum("kcr,rl->klc", crossed, inverse_cat, precision=FAST)
        parts = lax.all_to_all(lagged, "tm", split_axis=0, concat_axis=0, tiled=True)
        return jnp.sum(parts, axis=0, keepdims=True)

    first = finish(even)
    second = finish(odd)
    return jnp.concatenate([first, second], axis=0)


def solution(mesh):
    placed = (P("tm", "chan", None), P(), P())
    return jax.shard_map(
        per_device, mesh=mesh, in_specs=placed, out_specs=P("tm", None, "chan"), check_vma=False
    )
```
